32 devices in a mesh: row: 8 (over y, x, core), col: 4 (over z).
Axes of the slice: x: 2, y: 2, z: 4, core: 2. Of those that a mesh axis runs over, the one named last changes fastest.
Arguments:
- emb_in: float32 [16384, 128], P(('row', 'col')), may hold values from -2.5 to 2.5
- ctx_in: float32 [16384, 128], P(('row', 'col')), may hold values from -2.5 to 2.5
- pos_weight: bfloat16 [8, 4, 64, 256, 256], P('row', 'col'), may hold values from 0.049804688 to 3
- neg_weight: bfloat16 [8, 4, 64, 256, 256], P('row', 'col'), may hold values from 0.049804688 to 1
- tile_row: int32 [8, 4, 64], P('row', 'col'), may hold values from 0 to 7, as said below
- tile_col: int32 [8, 4, 64], P('row', 'col'), may hold values from 0 to 15, as said below
- tile_count: int32 [8, 4], P('row', 'col'), may hold values from 8 to 64, as said below
Outputs:
- emb_out: float32 [16384, 128], P(('row', 'col'))
- ctx_out: float32 [16384, 128], P(('row', 'col'))
The draws below stay inside these ranges and needn't reach their ends.
Inputs may be any that keep to these rules, and one draw needn't show every extreme that they name: `tile_row`: on each block the 64 slots name distinct tiles. `tile_col`: on each block the 64 slots name distinct tiles. `tile_count`: some block has all 64 slots live.
All inputs are finite; a program needn't handle non-finite values.
Results may differ from the reference program's by a relative error of at most 0.02.
Values may be sent and summed in bfloat16 or wider, within the bound.
No kernel may reach another device: no remote copies, remote signals or barrier semaphores. Data moves between devices by JAX's collectives and lax.ppermute only.
A program may use at most 128 MiB of HBM per device.

```python
import math
import jax
import jax.numpy as jnp
from jax import lax

DIM = 128
TILE = 256
SLICE = 512
CAP = 64
ITERS = 2
NODES = 16384
ROW_BLOCK = 2048
COL_BLOCK = 4096
ROW_TILES = 8
COL_TILES = 16
N_ROW = 8
N_COL = 4


def picked_tiles(key):
    inner = jax.random.fold_in(key, 7)
    keys = jax.random.split(inner, N_ROW * N_COL)
    picks = jax.vmap(lambda single: jax.random.permutation(single, ROW_TILES * COL_TILES)[:CAP])(keys)
    return picks.reshape(N_ROW, N_COL, CAP).astype(jnp.int32)


def draw_tile_row(key, part):
    return (picked_tiles(key) // COL_TILES).astype(jnp.int32)


def draw_tile_col(key, part):
    return (picked_tiles(key) % COL_TILES).astype(jnp.int32)


def draw_tile_count(key, part):
    inner = jax.random.fold_in(key, 11)
    first, second = jax.random.split(inner)
    drawn = jax.random.randint(first, (N_ROW * N_COL,), 0, CAP + 1, dtype=jnp.int32)
    counts = jnp.maximum(CAP // 8, drawn * drawn // CAP)
    busiest = jax.random.randint(second, (), 0, N_ROW * N_COL, dtype=jnp.int32)
    counts = jnp.where(jnp.arange(N_ROW * N_COL, dtype=jnp.int32) == busiest, CAP, counts)
    return counts.reshape(N_ROW, N_COL).astype(jnp.int32)


def level_of(stream_key, shape, pieces, least, top_value):
    factor_of = 1.0
    for axis_at, shards_of in pieces:
        heights = jax.random.uniform(jax.random.fold_in(jax.random.fold_in(stream_key, 6), axis_at), (shards_of,), jnp.float32, least / len(pieces), top_value / len(pieces))
        factor_of = factor_of * jnp.repeat(jnp.exp(heights), shape[axis_at] // shards_of).reshape((-1,) + (1,) * (len(shape) - 1 - axis_at))
    return factor_of


def gaussian(own_key, dims, width, reach, cuts=(), held_as=jnp.bfloat16):
    entries = width * jax.random.normal(own_key, dims, jnp.float32)
    if cuts:
        entries = entries * level_of(own_key, dims, cuts, -0.22, 0.18)
    return jnp.clip(entries, -reach, reach).astype(held_as)


def setup_inputs(seed: int = 0) -> dict:
    key_list = jax.random.split(jax.random.key(seed), 8)
    emb_in = gaussian(key_list[0], (NODES, DIM), 0.3, 2.5, ((0, 32),), jnp.float32)
    ctx_in = gaussian(key_list[1], (NODES, DIM), 0.3, 2.5, ((0, 32),), jnp.float32)
    pos_weight = jnp.clip(jnp.exp(math.log(3.0) - 4.0982585 * jax.random.uniform(key_list[2], (N_ROW, N_COL, CAP, TILE, TILE), jnp.float32) ** level_of(key_list[2], (N_ROW, N_COL, CAP, TILE, TILE), ((0, 8), (1, 4)), -0.2, 0.2)), 0.049804688, 3.0).astype(jnp.bfloat16)
    neg_weight = jnp.clip(jnp.exp(math.log(1.0) - 2.9996462 * jax.random.uniform(key_list[3], (N_ROW, N_COL, CAP, TILE, TILE), jnp.float32) ** level_of(key_list[3], (N_ROW, N_COL, CAP, TILE, TILE), ((0, 8), (1, 4)), -0.2, 0.2)), 0.049804688, 1.0).astype(jnp.bfloat16)
    tile_row = draw_tile_row(jax.random.fold_in(key_list[7], 71), 0)
    tile_col = draw_tile_col(jax.random.fold_in(key_list[7], 71), 0)
    tile_count = draw_tile_count(jax.random.fold_in(key_list[7], 71), 0)
    return {"emb_in": emb_in, "ctx_in": ctx_in, "pos_weight": pos_weight, "neg_weight": neg_weight, "tile_row": tile_row, "tile_col": tile_col, "tile_count": tile_count}


def tile_sweep(pos, neg, rows, cols, count, emb_low, ctx_low):
    tile_size = pos.shape[-1]

    def visit(slot_index, totals):
        grad_emb, grad_ctx = totals
        row_start = (rows[slot_index] * tile_size).astype(jnp.int32)
        col_start = (cols[slot_index] * tile_size).astype(jnp.int32)
        emb_rows = lax.dynamic_slice_in_dim(emb_low, row_start, tile_size, 0)
        ctx_rows = lax.dynamic_slice_in_dim(ctx_low, col_start, tile_size, 0)
        score = lax.dot_general(emb_rows, ctx_rows, (((1,), (1,)), ((), ())), preferred_element_type=jnp.float32)
        squashed = jax.nn.sigmoid(score)
        positive = lax.dynamic_index_in_dim(pos, slot_index, 0, keepdims=False).astype(jnp.float32)
        negative = lax.dynamic_index_in_dim(neg, slot_index, 0, keepdims=False).astype(jnp.float32)
        coeff_tile = (positive * (1.0 - squashed) - negative * squashed).astype(jnp.bfloat16)
        emb_step = jnp.dot(coeff_tile, ctx_rows, preferred_element_type=jnp.float32)
        ctx_step = lax.dot_general(coeff_tile, emb_rows, (((0,), (0,)), ((), ())), preferred_element_type=jnp.float32)
        grad_emb = lax.dynamic_update_slice_in_dim(grad_emb, lax.dynamic_slice_in_dim(grad_emb, row_start, tile_size, 0) + emb_step, row_start, 0)
        grad_ctx = lax.dynamic_update_slice_in_dim(grad_ctx, lax.dynamic_slice_in_dim(grad_ctx, col_start, tile_size, 0) + ctx_step, col_start, 0)
        return grad_emb, grad_ctx

    start = (jnp.zeros(emb_low.shape, jnp.float32), jnp.zeros(ctx_low.shape, jnp.float32))
    return lax.fori_loop(jnp.int32(0), count.astype(jnp.int32), visit, start)


def reference(emb_in, ctx_in, pos_weight, neg_weight, tile_row, tile_col, tile_count):
    emb = emb_in
    ctx = ctx_in
    for iteration in range(ITERS):
        emb_low = emb.astype(jnp.bfloat16).reshape(N_ROW, ROW_BLOCK, DIM)
        ctx_low = ctx.astype(jnp.bfloat16).reshape(N_ROW, N_COL, SLICE, DIM).transpose(1, 0, 2, 3).reshape(N_COL, COL_BLOCK, DIM)

        def per_device(device, totals):
            grad_emb, grad_ctx = totals
            device = device.astype(jnp.int32)
            row_index = device // N_COL
            col_index = device % N_COL
            emb_block = lax.dynamic_index_in_dim(emb_low, row_index, 0, keepdims=False)
            ctx_block = lax.dynamic_index_in_dim(ctx_low, col_index, 0, keepdims=False)
            pos = pos_weight[row_index, col_index]
            neg = neg_weight[row_index, col_index]
            part_emb, part_ctx = tile_sweep(pos, neg, tile_row[row_index, col_index], tile_col[row_index, col_index], tile_count[row_index, col_index], emb_block, ctx_block)
            part_emb = lax.optimization_barrier(part_emb.astype(jnp.bfloat16)).astype(jnp.float32)
            part_ctx = lax.optimization_barrier(part_ctx.astype(jnp.bfloat16)).astype(jnp.float32)
            grad_emb = grad_emb.at[row_index].add(part_emb)
            grad_ctx = grad_ctx.at[col_index].add(part_ctx)
            return grad_emb, grad_ctx

        start = (jnp.zeros((N_ROW, ROW_BLOCK, DIM), jnp.float32), jnp.zeros((N_COL, COL_BLOCK, DIM), jnp.float32))
        grad_emb, grad_ctx = lax.fori_loop(jnp.int32(0), jnp.int32(N_ROW * N_COL), per_device, start)
        emb = emb + 0.05 * grad_emb.reshape(NODES, DIM)
        ctx = ctx + 0.05 * grad_ctx.reshape(N_COL, N_ROW, SLICE, DIM).transpose(1, 0, 2, 3).reshape(NODES, DIM)
    return emb, ctx
```

```python
import functools

import jax
import jax.numpy as jnp
from jax import lax
from jax.experimental import pallas as pl
from jax.experimental.pallas import tpu as pltpu
from jax.sharding import PartitionSpec as P

ITERS = 2


def sweep_kernel(tile, rows_ref, cols_ref, count_ref, emb_ref, ctx_ref, pos_ref, neg_ref,
                 gemb_ref, gctx_ref, acc_e, acc_c):
    k = pl.program_id(0)
    n = count_ref[0]

    @pl.when(k == 0)
    def _():
        acc_e[...] = jnp.zeros_like(acc_e)
        acc_c[...] = jnp.zeros_like(acc_c)

    @pl.when(k < n)
    def _():
        r0 = pl.multiple_of(rows_ref[k] * tile, tile)
        c0 = pl.multiple_of(cols_ref[k] * tile, tile)
        e = emb_ref[pl.ds(r0, tile), :]
        c = ctx_ref[pl.ds(c0, tile), :]
        score = lax.dot_general(e, c, (((1,), (1,)), ((), ())), preferred_element_type=jnp.float32)
        squashed = jax.nn.sigmoid(score)
        positive = pos_ref[0].astype(jnp.float32)
        negative = neg_ref[0].astype(jnp.float32)
        coeff = (positive * (1.0 - squashed) - negative * squashed).astype(jnp.bfloat16)
        acc_e[pl.ds(r0, tile), :] += jnp.dot(coeff, c, preferred_element_type=jnp.float32)
        acc_c[pl.ds(c0, tile), :] += lax.dot_general(
            coeff, e, (((0,), (0,)), ((), ())), preferred_element_type=jnp.float32
        )

    @pl.when(k == pl.num_programs(0) - 1)
    def _():
        gemb_ref[...] = acc_e[...].astype(gemb_ref.dtype)
        gctx_ref[...] = acc_c[...].astype(gctx_ref.dtype)


def tile_sweep(pos, neg, rows, cols, count, emb_low, ctx_low):
    cap, tile, _ = pos.shape
    ne, dim = emb_low.shape
    nc = ctx_low.shape[0]

    def slot(k, rows_ref, cols_ref, count_ref):
        return (jnp.minimum(k, jnp.maximum(count_ref[0] - 1, 0)), 0, 0)

    grid_spec = pltpu.PrefetchScalarGridSpec(
        num_scalar_prefetch=3,
        grid=(cap,),
        in_specs=[
            pl.BlockSpec((ne, dim), lambda k, *_: (0, 0)),
            pl.BlockSpec((nc, dim), lambda k, *_: (0, 0)),
            pl.BlockSpec((1, tile, tile), slot),
            pl.BlockSpec((1, tile, tile), slot),
        ],
        out_specs=[
            pl.BlockSpec((ne, dim), lambda k, *_: (0, 0)),
            pl.BlockSpec((nc, dim), lambda k, *_: (0, 0)),
        ],
        scratch_shapes=[
            pltpu.VMEM((ne, dim), jnp.float32),
            pltpu.VMEM((nc, dim), jnp.float32),
        ],
    )
    flops = cap * 3 * 2 * tile * tile * dim
    return pl.pallas_call(
        functools.partial(sweep_kernel, tile),
        grid_spec=grid_spec,
        out_shape=(
            jax.ShapeDtypeStruct((ne, dim), jnp.bfloat16),
            jax.ShapeDtypeStruct((nc, dim), jnp.bfloat16),
        ),
        compiler_params=pltpu.CompilerParams(dimension_semantics=("arbitrary",)),
        cost_estimate=pl.CostEstimate(
            flops=flops,
            transcendentals=cap * tile * tile,
            bytes_accessed=2 * cap * tile * tile * 2 + 3 * (ne + nc) * dim * 2,
        ),
    )(rows, cols, count.reshape(1), emb_low, ctx_low, pos, neg)


def body(emb_in, ctx_in, pos_weight, neg_weight, tile_row, tile_col, tile_count):
    pos = pos_weight[0, 0]
    neg = neg_weight[0, 0]
    rows = tile_row[0, 0]
    cols = tile_col[0, 0]
    count = tile_count[0, 0]
    emb = emb_in
    ctx = ctx_in
    for iteration in range(ITERS):
        emb_low = lax.all_gather(emb.astype(jnp.bfloat16), "col", axis=0, tiled=True)
        ctx_low = lax.all_gather(ctx.astype(jnp.bfloat16), "row", axis=0, tiled=True)
        grad_emb, grad_ctx = tile_sweep(pos, neg, rows, cols, count, emb_low, ctx_low)
        emb = emb + 0.05 * lax.psum_scatter(
            grad_emb, "col", scatter_dimension=0, tiled=True
        ).astype(jnp.float32)
        ctx = ctx + 0.05 * lax.psum_scatter(
            grad_ctx, "row", scatter_dimension=0, tiled=True
        ).astype(jnp.float32)
    return (emb, ctx)


def solution(mesh):
    in_specs = (
        P(("row", "col"), None),
        P(("row", "col"), None),
        P("row", "col", None, None, None),
        P("row", "col", None, None, None),
        P("row", "col", None),
        P("row", "col", None),
        P("row", "col"),
    )
    out_specs = (P(("row", "col"), None), P(("row", "col"), None))
    return jax.shard_map(body, mesh=mesh, in_specs=in_specs, out_specs=out_specs, check_vma=False)
```

```python
import functools

import jax
import jax.numpy as jnp
from jax import lax
from jax.experimental import pallas as pl
from jax.experimental.pallas import tpu as pltpu
from jax.sharding import PartitionSpec as P

ITERS = 2


def sweep_kernel(tile, rows_ref, cols_ref, count_ref, emb_ref, ctx_ref, pos_ref, neg_ref,
                 gemb_ref, gctx_ref, acc_e, acc_c):
    k = pl.program_id(0)
    n = count_ref[0]

    @pl.when(k == 0)
    def _():
        acc_e[...] = jnp.zeros_like(acc_e)
        acc_c[...] = jnp.zeros_like(acc_c)

    @pl.when(k < n)
    def _():
        r0 = pl.multiple_of(rows_ref[k] * tile, tile)
        c0 = pl.multiple_of(cols_ref[k] * tile, tile)
        e = emb_ref[pl.ds(r0, tile), :]
        c = ctx_ref[pl.ds(c0, tile), :]
        score = lax.dot_general(e, c, (((1,), (1,)), ((), ())), preferred_element_type=jnp.float32)
        squashed = jax.nn.sigmoid(score)
        positive = pos_ref[0].astype(jnp.float32)
        negative = neg_ref[0].astype(jnp.float32)
        coeff = (positive * (1.0 - squashed) - negative * squashed).astype(jnp.bfloat16)
        acc_e[pl.ds(r0, tile), :] += jnp.dot(coeff, c, preferred_element_type=jnp.float32)
        acc_c[pl.ds(c0, tile), :] += lax.dot_general(
            coeff, e, (((0,), (0,)), ((), ())), preferred_element_type=jnp.float32
        )

    @pl.when(k == pl.num_programs(0) - 1)
    def _():
        gemb_ref[...] = acc_e[...].astype(gemb_ref.dtype)
        gctx_ref[...] = acc_c[...].astype(gctx_ref.dtype)


def tile_sweep(pos, neg, rows, cols, count, emb_low, ctx_low):
    cap, tile, _ = pos.shape
    ne, dim = emb_low.shape
    nc = ctx_low.shape[0]

    def slot(k, rows_ref, cols_ref, count_ref):
        return (jnp.minimum(k, jnp.maximum(count_ref[0] - 1, 0)), 0, 0)

    grid_spec = pltpu.PrefetchScalarGridSpec(
        num_scalar_prefetch=3,
        grid=(cap,),
        in_specs=[
            pl.BlockSpec((ne, dim), lambda k, *_: (0, 0)),
            pl.BlockSpec((nc, dim), lambda k, *_: (0, 0)),
            pl.BlockSpec((1, tile, tile), slot),
            pl.BlockSpec((1, tile, tile), slot),
        ],
        out_specs=[
            pl.BlockSpec((ne, dim), lambda k, *_: (0, 0)),
            pl.BlockSpec((nc, dim), lambda k, *_: (0, 0)),
        ],
        scratch_shapes=[
            pltpu.VMEM((ne, dim), jnp.float32),
            pltpu.VMEM((nc, dim), jnp.float32),
        ],
    )
    flops = cap * 3 * 2 * tile * tile * dim
    return pl.pallas_call(
        functools.partial(sweep_kernel, tile),
        grid_spec=grid_spec,
        out_shape=(
            jax.ShapeDtypeStruct((ne, dim), jnp.bfloat16),
            jax.ShapeDtypeStruct((nc, dim), jnp.bfloat16),
        ),
        compiler_params=pltpu.CompilerParams(dimension_semantics=("arbitrary",)),
        cost_estimate=pl.CostEstimate(
            flops=flops,
            transcendentals=cap * tile * tile,
            bytes_accessed=2 * cap * tile * tile * 2 + 3 * (ne + nc) * dim * 2,
        ),
    )(rows, cols, count.reshape(1), emb_low, ctx_low, pos, neg)


def gather_rotated(x, axis, n):
    pieces = [x]
    for s in range(1, n):
        pieces.append(lax.ppermute(x, axis, [(i, (i + s) % n) for i in range(n)]))
    return jnp.concatenate(pieces, axis=0)


def scatter_rotated(g, axis, n):
    chunks = g.reshape(n, -1, g.shape[-1])
    total = chunks[0].astype(jnp.float32)
    for s in range(1, n):
        got = lax.ppermute(chunks[(n - s) % n], axis, [(i, (i + s) % n) for i in range(n)])
        total = total + got.astype(jnp.float32)
    return total


def rotate_index(index, me, n, per_run):
    run = index // per_run
    return ((me - run) % n) * per_run + index % per_run


def body(emb_in, ctx_in, pos_weight, neg_weight, tile_row, tile_col, tile_count):
    n_row = lax.axis_size("row")
    n_col = lax.axis_size("col")
    me_row = lax.axis_index("row")
    me_col = lax.axis_index("col")
    pos = pos_weight[0, 0]
    neg = neg_weight[0, 0]
    tile = pos.shape[-1]
    per_run = emb_in.shape[0] // tile
    rows = rotate_index(tile_row[0, 0], me_col, n_col, per_run)
    cols = rotate_index(tile_col[0, 0], me_row, n_row, per_run)
    count = tile_count[0, 0]
    emb = emb_in
    ctx = ctx_in
    for iteration in range(ITERS):
        emb_low = gather_rotated(emb.astype(jnp.bfloat16), "col", n_col)
        ctx_low = gather_rotated(ctx.astype(jnp.bfloat16), "row", n_row)
        grad_emb, grad_ctx = tile_sweep(pos, neg, rows, cols, count, emb_low, ctx_low)
        emb = emb + 0.05 * scatter_rotated(grad_emb, "col", n_col)
        ctx = ctx + 0.05 * scatter_rotated(grad_ctx, "row", n_row)
    return (emb, ctx)


def solution(mesh):
    in_specs = (
        P(("row", "col"), None),
        P(("row", "col"), None),
        P("row", "col", None, None, None),
        P("row", "col", None, None, None),
        P("row", "col", None),
        P("row", "col", None),
        P("row", "col"),
    )
    out_specs = (P(("row", "col"), None), P(("row", "col"), None))
    return jax.shard_map(body, mesh=mesh, in_specs=in_specs, out_specs=out_specs, check_vma=False)
```

```python
import functools

import jax
import jax.numpy as jnp
from jax import lax
from jax.experimental import pallas as pl
from jax.experimental.pallas import tpu as pltpu
from jax.sharding import PartitionSpec as P

ITERS = 2


def sweep_kernel(tile, group, rows_ref, cols_ref, count_ref, emb_ref, embt_ref, ctx_ref, pos_ref, neg_ref,
                 gemb_ref, gctxt_ref, acc_e, acc_ct):
    k = pl.program_id(0)
    n = count_ref[0]

    @pl.when(k == 0)
    def _():
        acc_e[...] = jnp.zeros_like(acc_e)
        acc_ct[...] = jnp.zeros_like(acc_ct)

    def visit(j):
        slot = k * group + j
        r0 = pl.multiple_of(rows_ref[slot] * tile, tile)
        c0 = pl.multiple_of(cols_ref[slot] * tile, tile)
        e = emb_ref[pl.ds(r0, tile), :]
        c = ctx_ref[pl.ds(c0, tile), :]
        score = lax.dot_general(e, c, (((1,), (1,)), ((), ())), preferred_element_type=jnp.float32)
        positive = pos_ref[j].astype(jnp.float32)
        negative = neg_ref[j].astype(jnp.float32)
        t = jnp.tanh(score * 0.5)
        coeff = (0.5 * ((positive - negative) - (positive + negative) * t)).astype(jnp.bfloat16)
        acc_e[pl.ds(r0, tile), :] += jnp.dot(coeff, c, preferred_element_type=jnp.float32)
        acc_ct[:, pl.ds(c0, tile)] += jnp.dot(
            embt_ref[:, pl.ds(r0, tile)], coeff, preferred_element_type=jnp.float32
        )

    full = (k + 1) * group <= n

    @pl.when(full)
    def _():
        for j in range(group):
            visit(j)

    @pl.when(jnp.logical_not(full))
    def _():
        for j in range(group):
            pl.when(k * group + j < n)(functools.partial(visit, j))

    @pl.when(k == pl.num_programs(0) - 1)
    def _():
        gemb_ref[...] = acc_e[...].astype(gemb_ref.dtype)
        gctxt_ref[...] = acc_ct[...].astype(gctxt_ref.dtype)


def tile_sweep(pos, neg, rows, cols, count, emb_low, ctx_low):
    cap, tile, _ = pos.shape
    ne, dim = emb_low.shape
    nc = ctx_low.shape[0]
    group = next(g for g in (8, 4, 2, 1) if cap % g == 0)

    def slot(k, rows_ref, cols_ref, count_ref):
        last = jnp.maximum((count_ref[0] + group - 1) // group - 1, 0)
        return (jnp.minimum(k, last), 0, 0)

    grid_spec = pltpu.PrefetchScalarGridSpec(
        num_scalar_prefetch=3,
        grid=(cap // group,),
        in_specs=[
            pl.BlockSpec((ne, dim), lambda k, *_: (0, 0)),
            pl.BlockSpec((dim, ne), lambda k, *_: (0, 0)),
            pl.BlockSpec((nc, dim), lambda k, *_: (0, 0)),
            pl.BlockSpec((group, tile, tile), slot),
            pl.BlockSpec((group, tile, tile), slot),
        ],
        out_specs=[
            pl.BlockSpec((ne, dim), lambda k, *_: (0, 0)),
            pl.BlockSpec((dim, nc), lambda k, *_: (0, 0)),
        ],
        scratch_shapes=[
            pltpu.VMEM((ne, dim), jnp.float32),
            pltpu.VMEM((dim, nc), jnp.float32),
        ],
    )
    flops = cap * 3 * 2 * tile * tile * dim
    return pl.pallas_call(
        functools.partial(sweep_kernel, tile, group),
        grid_spec=grid_spec,
        out_shape=(
            jax.ShapeDtypeStruct((ne, dim), jnp.bfloat16),
            jax.ShapeDtypeStruct((dim, nc), jnp.bfloat16),
        ),
        compiler_params=pltpu.CompilerParams(dimension_semantics=("arbitrary",)),
        cost_estimate=pl.CostEstimate(
            flops=flops,
            transcendentals=cap * tile * tile,
            bytes_accessed=2 * cap * tile * tile * 2 + 3 * (ne + nc) * dim * 2,
        ),
    )(rows, cols, count.reshape(1), emb_low, emb_low.T, ctx_low, pos, neg)


def gather_rotated(x, axis, n):
    pieces = [x]
    for s in range(1, n):
        pieces.append(lax.ppermute(x, axis, [(i, (i + s) % n) for i in range(n)]))
    return jnp.concatenate(pieces, axis=0)


def scatter_rotated(g, axis, n):
    chunks = g.reshape(n, -1, g.shape[-1])
    total = chunks[0].astype(jnp.float32)
    for s in range(1, n):
        got = lax.ppermute(chunks[(n - s) % n], axis, [(i, (i + s) % n) for i in range(n)])
        total = total + got.astype(jnp.float32)
    return total


def scatter_rotated_t(gt, axis, n):
    width = gt.shape[1] // n
    chunk = lambda s: gt[:, s * width:(s + 1) * width]
    total = chunk(0).astype(jnp.float32)
    for s in range(1, n):
        got = lax.ppermute(chunk((n - s) % n), axis, [(i, (i + s) % n) for i in range(n)])
        total = total + got.astype(jnp.float32)
    return total.T


def rotate_index(index, me, n, per_run):
    run = index // per_run
    return ((me - run) % n) * per_run + index % per_run


def body(emb_in, ctx_in, pos_weight, neg_weight, tile_row, tile_col, tile_count):
    n_row = lax.axis_size("row")
    n_col = lax.axis_size("col")
    me_row = lax.axis_index("row")
    me_col = lax.axis_index("col")
    pos = pos_weight[0, 0]
    neg = neg_weight[0, 0]
    tile = pos.shape[-1]
    per_run = emb_in.shape[0] // tile
    rows = rotate_index(tile_row[0, 0], me_col, n_col, per_run)
    cols = rotate_index(tile_col[0, 0], me_row, n_row, per_run)
    count = tile_count[0, 0]
    emb = emb_in
    ctx = ctx_in
    for iteration in range(ITERS):
        emb_low = gather_rotated(emb.astype(jnp.bfloat16), "col", n_col)
        ctx_low = gather_rotated(ctx.astype(jnp.bfloat16), "row", n_row)
        grad_emb, grad_ctx_t = tile_sweep(pos, neg, rows, cols, count, emb_low, ctx_low)
        emb = emb + 0.05 * scatter_rotated(grad_emb, "col", n_col)
        ctx = ctx + 0.05 * scatter_rotated_t(grad_ctx_t, "row", n_row)
    return (emb, ctx)


def solution(mesh):
    in_specs = (
        P(("row", "col"), None),
        P(("row", "col"), None),
        P("row", "col", None, None, None),
        P("row", "col", None, None, None),
        P("row", "col", None),
        P("row", "col", None),
        P("row", "col"),
    )
    out_specs = (P(("row", "col"), None), P(("row", "col"), None))
    return jax.shard_map(body, mesh=mesh, in_specs=in_specs, out_specs=out_specs, check_vma=False)
```

```python
import functools

import jax
import jax.numpy as jnp
from jax import lax
from jax.experimental import pallas as pl
from jax.experimental.pallas import tpu as pltpu
from jax.sharding import PartitionSpec as P

ITERS = 2


def sweep_kernel(tile, group, rows_ref, cols_ref, count_ref, emb_ref, embt_ref, ctx_ref, pos_ref, neg_ref,
                 gemb_ref, gctxt_ref, acc_e, acc_ct):
    k = pl.program_id(0)
    n = count_ref[0]

    @pl.when(k == 0)
    def _():
        acc_e[...] = jnp.zeros_like(acc_e)
        acc_ct[...] = jnp.zeros_like(acc_ct)

    def visit(j):
        slot = k * group + j
        r0 = pl.multiple_of(rows_ref[slot] * tile, tile)
        c0 = pl.multiple_of(cols_ref[slot] * tile, tile)
        e = emb_ref[pl.ds(r0, tile), :]
        c = ctx_ref[pl.ds(c0, tile), :]
        score = lax.dot_general(e, c, (((1,), (1,)), ((), ())), preferred_element_type=jnp.float32)
        positive = pos_ref[j].astype(jnp.float32)
        negative = neg_ref[j].astype(jnp.float32)
        t = jnp.tanh(score * 0.5)
        coeff = (0.5 * ((positive - negative) - (positive + negative) * t)).astype(jnp.bfloat16)
        acc_e[pl.ds(r0, tile), :] += jnp.dot(coeff, c, preferred_element_type=jnp.float32)
        acc_ct[:, pl.ds(c0, tile)] += jnp.dot(
            embt_ref[:, pl.ds(r0, tile)], coeff, preferred_element_type=jnp.float32
        )

    full = (k + 1) * group <= n

    @pl.when(full)
    def _():
        for j in range(group):
            visit(j)

    @pl.when(jnp.logical_not(full))
    def _():
        for j in range(group):
            pl.when(k * group + j < n)(functools.partial(visit, j))

    @pl.when(k == pl.num_programs(0) - 1)
    def _():
        gemb_ref[...] = acc_e[...].astype(gemb_ref.dtype)
        gctxt_ref[...] = acc_ct[...].astype(gctxt_ref.dtype)


def tile_sweep(pos, neg, rows, cols, count, emb_low, ctx_low):
    cap, tile, _ = pos.shape
    ne, dim = emb_low.shape
    nc = ctx_low.shape[0]
    group = next(g for g in (8, 4, 2, 1) if cap % g == 0)

    def slot(k, rows_ref, cols_ref, count_ref):
        last = jnp.maximum((count_ref[0] + group - 1) // group - 1, 0)
        return (jnp.minimum(k, last), 0, 0)

    grid_spec = pltpu.PrefetchScalarGridSpec(
        num_scalar_prefetch=3,
        grid=(cap // group,),
        in_specs=[
            pl.BlockSpec((ne, dim), lambda k, *_: (0, 0)),
            pl.BlockSpec((dim, ne), lambda k, *_: (0, 0)),
            pl.BlockSpec((nc, dim), lambda k, *_: (0, 0)),
            pl.BlockSpec((group, tile, tile), slot),
            pl.BlockSpec((group, tile, tile), slot),
        ],
        out_specs=[
            pl.BlockSpec((ne, dim), lambda k, *_: (0, 0)),
            pl.BlockSpec((dim, nc), lambda k, *_: (0, 0)),
        ],
        scratch_shapes=[
            pltpu.VMEM((ne, dim), jnp.float32),
            pltpu.VMEM((dim, nc), jnp.float32),
        ],
    )
    flops = cap * 3 * 2 * tile * tile * dim
    return pl.pallas_call(
        functools.partial(sweep_kernel, tile, group),
        grid_spec=grid_spec,
        out_shape=(
            jax.ShapeDtypeStruct((ne, dim), jnp.bfloat16),
            jax.ShapeDtypeStruct((dim, nc), jnp.bfloat16),
        ),
        compiler_params=pltpu.CompilerParams(dimension_semantics=("arbitrary",)),
        cost_estimate=pl.CostEstimate(
            flops=flops,
            transcendentals=cap * tile * tile,
            bytes_accessed=2 * cap * tile * tile * 2 + 3 * (ne + nc) * dim * 2,
        ),
    )(rows, cols, count.reshape(1), emb_low, emb_low.T, ctx_low, pos, neg)


def gather_rotated(x, axis, n):
    pieces = [x]
    for s in range(1, n):
        pieces.append(lax.ppermute(x, axis, [(i, (i + s) % n) for i in range(n)]))
    return jnp.concatenate(pieces, axis=0)


def scatter_rotated(g, axis, n):
    chunks = g.reshape(n, -1, g.shape[-1])
    total = chunks[0].astype(jnp.float32)
    for s in range(1, n):
        got = lax.ppermute(chunks[(n - s) % n], axis, [(i, (i + s) % n) for i in range(n)])
        total = total + got.astype(jnp.float32)
    return total


def scatter_rotated_t(gt, axis, n):
    width = gt.shape[1] // n
    chunk = lambda s: gt[:, s * width:(s + 1) * width]
    total = chunk(0).astype(jnp.float32)
    for s in range(1, n):
        got = lax.ppermute(chunk((n - s) % n), axis, [(i, (i + s) % n) for i in range(n)])
        total = total + got.astype(jnp.float32)
    return total.T


def paired(n):
    return n % 2 == 0 and n & (n - 1) == 0


def gather_paired(x, axis, n):
    pair = jnp.concatenate([x, lax.ppermute(x, axis, [(i, i ^ 1) for i in range(n)])], axis=0)
    blocks = [pair]
    for b in range(1, n // 2):
        blocks.append(lax.ppermute(pair, axis, [(i, i ^ (2 * b)) for i in range(n)]))
    return jnp.concatenate(blocks, axis=0)


def scatter_paired_t(gt, axis, n):
    width = gt.shape[1] // n
    total = gt[:, : 2 * width].astype(jnp.float32)
    for b in range(1, n // 2):
        got = lax.ppermute(
            gt[:, 2 * b * width : (2 * b + 2) * width], axis, [(i, i ^ (2 * b)) for i in range(n)]
        )
        total = total + got.astype(jnp.float32)
    got = lax.ppermute(total[:, width:], axis, [(i, i ^ 1) for i in range(n)])
    return (total[:, :width] + got).T


def pair_index(index, me, per_run):
    return (me ^ (index // per_run)) * per_run + index % per_run


def rotate_index(index, me, n, per_run):
    run = index // per_run
    return ((me - run) % n) * per_run + index % per_run


def body(emb_in, ctx_in, pos_weight, neg_weight, tile_row, tile_col, tile_count):
    n_row = lax.axis_size("row")
    n_col = lax.axis_size("col")
    me_row = lax.axis_index("row")
    me_col = lax.axis_index("col")
    pos = pos_weight[0, 0]
    neg = neg_weight[0, 0]
    tile = pos.shape[-1]
    per_run = emb_in.shape[0] // tile
    rows = rotate_index(tile_row[0, 0], me_col, n_col, per_run)
    if paired(n_row):
        cols = pair_index(tile_col[0, 0], me_row, per_run)
        gather_row, scatter_row = gather_paired, scatter_paired_t
    else:
        cols = rotate_index(tile_col[0, 0], me_row, n_row, per_run)
        gather_row, scatter_row = gather_rotated, scatter_rotated_t
    count = tile_count[0, 0]
    emb = emb_in
    ctx = ctx_in
    for iteration in range(ITERS):
        emb_low = gather_rotated(emb.astype(jnp.bfloat16), "col", n_col)
        ctx_low = gather_row(ctx.astype(jnp.bfloat16), "row", n_row)
        grad_emb, grad_ctx_t = tile_sweep(pos, neg, rows, cols, count, emb_low, ctx_low)
        emb = emb + 0.05 * scatter_rotated(grad_emb, "col", n_col)
        ctx = ctx + 0.05 * scatter_row(grad_ctx_t, "row", n_row)
    return (emb, ctx)


def solution(mesh):
    in_specs = (
        P(("row", "col"), None),
        P(("row", "col"), None),
        P("row", "col", None, None, None),
        P("row", "col", None, None, None),
        P("row", "col", None),
        P("row", "col", None),
        P("row", "col"),
    )
    out_specs = (P(("row", "col"), None), P(("row", "col"), None))
    return jax.shard_map(body, mesh=mesh, in_specs=in_specs, out_specs=out_specs, check_vma=False)
```

```python
import functools

import jax
import jax.numpy as jnp
from jax import lax
from jax.experimental import pallas as pl
from jax.experimental.pallas import tpu as pltpu
from jax.sharding import PartitionSpec as P

ITERS = 2


def sweep_kernel(tile, group, rows_ref, cols_ref, count_ref, emb_ref, embt_ref, ctx_ref, pos_ref, neg_ref,
                 gemb_ref, gctxt_ref, acc_e, acc_ct):
    k = pl.program_id(0)
    n = count_ref[0]

    @pl.when(k == 0)
    def _():
        acc_e[...] = jnp.zeros_like(acc_e)
        acc_ct[...] = jnp.zeros_like(acc_ct)

    def visit(j):
        slot = k * group + j
        r0 = pl.multiple_of(rows_ref[slot] * tile, tile)
        c0 = pl.multiple_of(cols_ref[slot] * tile, tile)
        e = emb_ref[pl.ds(r0, tile), :]
        c = ctx_ref[pl.ds(c0, tile), :]
        score = lax.dot_general(e, c, (((1,), (1,)), ((), ())), preferred_element_type=jnp.float32)
        positive = pos_ref[j].astype(jnp.float32)
        negative = neg_ref[j].astype(jnp.float32)
        t = jnp.tanh(score * 0.5)
        coeff = (0.5 * ((positive - negative) - (positive + negative) * t)).astype(jnp.bfloat16)
        acc_e[pl.ds(r0, tile), :] += jnp.dot(coeff, c, preferred_element_type=jnp.float32)
        acc_ct[:, pl.ds(c0, tile)] += jnp.dot(
            embt_ref[:, pl.ds(r0, tile)], coeff, preferred_element_type=jnp.float32
        )

    full = (k + 1) * group <= n

    @pl.when(full)
    def _():
        for j in range(group):
            visit(j)

    @pl.when(jnp.logical_not(full))
    def _():
        for j in range(group):
            pl.when(k * group + j < n)(functools.partial(visit, j))

    @pl.when(k == pl.num_programs(0) - 1)
    def _():
        gemb_ref[...] = acc_e[...].astype(gemb_ref.dtype)
        gctxt_ref[...] = acc_ct[...].astype(gctxt_ref.dtype)


def tile_sweep(pos, neg, rows, cols, count, emb_low, ctx_low):
    cap, tile, _ = pos.shape
    ne, dim = emb_low.shape
    nc = ctx_low.shape[0]
    group = next(g for g in (8, 4, 2, 1) if cap % g == 0)

    def slot(k, rows_ref, cols_ref, count_ref):
        last = jnp.maximum((count_ref[0] + group - 1) // group - 1, 0)
        return (jnp.minimum(k, last), 0, 0)

    grid_spec = pltpu.PrefetchScalarGridSpec(
        num_scalar_prefetch=3,
        grid=(cap // group,),
        in_specs=[
            pl.BlockSpec((ne, dim), lambda k, *_: (0, 0)),
            pl.BlockSpec((dim, ne), lambda k, *_: (0, 0)),
            pl.BlockSpec((nc, dim), lambda k, *_: (0, 0)),
            pl.BlockSpec((group, tile, tile), slot),
            pl.BlockSpec((group, tile, tile), slot),
        ],
        out_specs=[
            pl.BlockSpec((ne, dim), lambda k, *_: (0, 0)),
            pl.BlockSpec((dim, nc), lambda k, *_: (0, 0)),
        ],
        scratch_shapes=[
            pltpu.VMEM((ne, dim), jnp.float32),
            pltpu.VMEM((dim, nc), jnp.float32),
        ],
    )
    flops = cap * 3 * 2 * tile * tile * dim
    return pl.pallas_call(
        functools.partial(sweep_kernel, tile, group),
        grid_spec=grid_spec,
        out_shape=(
            jax.ShapeDtypeStruct((ne, dim), jnp.bfloat16),
            jax.ShapeDtypeStruct((dim, nc), jnp.bfloat16),
        ),
        compiler_params=pltpu.CompilerParams(dimension_semantics=("arbitrary",)),
        cost_estimate=pl.CostEstimate(
            flops=flops,
            transcendentals=cap * tile * tile,
            bytes_accessed=2 * cap * tile * tile * 2 + 3 * (ne + nc) * dim * 2,
        ),
    )(rows, cols, count.reshape(1), emb_low, emb_low.T, ctx_low, pos, neg)


def gather_rotated(x, axis, n):
    pieces = [x]
    for s in range(1, n):
        pieces.append(lax.ppermute(x, axis, [(i, (i + s) % n) for i in range(n)]))
    return jnp.concatenate(pieces, axis=0)


def scatter_rotated(g, axis, n):
    chunks = g.reshape(n, -1, g.shape[-1])
    total = chunks[0].astype(jnp.float32)
    for s in range(1, n):
        got = lax.ppermute(chunks[(n - s) % n], axis, [(i, (i + s) % n) for i in range(n)])
        total = total + got.astype(jnp.float32)
    return total


def scatter_rotated_t(gt, axis, n):
    width = gt.shape[1] // n
    chunk = lambda s: gt[:, s * width:(s + 1) * width]
    total = chunk(0).astype(jnp.float32)
    for s in range(1, n):
        got = lax.ppermute(chunk((n - s) % n), axis, [(i, (i + s) % n) for i in range(n)])
        total = total + got.astype(jnp.float32)
    return total.T


def paired(n):
    return n % 2 == 0 and n & (n - 1) == 0


def gather_paired(x, axis, n):
    pair = jnp.concatenate([x, lax.ppermute(x, axis, [(i, i ^ 1) for i in range(n)])], axis=0)
    blocks = [pair]
    for b in range(1, n // 2):
        blocks.append(lax.ppermute(pair, axis, [(i, i ^ (2 * b)) for i in range(n)]))
    return jnp.concatenate(blocks, axis=0)


def scatter_paired_t(gt, axis, n):
    width = gt.shape[1] // n
    total = gt[:, : 2 * width].astype(jnp.float32)
    for b in range(1, n // 2):
        got = lax.ppermute(
            gt[:, 2 * b * width : (2 * b + 2) * width], axis, [(i, i ^ (2 * b)) for i in range(n)]
        )
        total = total + got.astype(jnp.float32)
    got = lax.ppermute(total[:, width:], axis, [(i, i ^ 1) for i in range(n)])
    return (total[:, :width] + got).T


def gather_xor(x, axis, n):
    pieces = [x]
    for p in range(1, n):
        pieces.append(lax.ppermute(x, axis, [(i, i ^ p) for i in range(n)]))
    return jnp.concatenate(pieces, axis=0)


def scatter_xor_t(gt, axis, n):
    width = gt.shape[1] // n
    total = gt[:, :width].astype(jnp.float32)
    for p in range(1, n):
        got = lax.ppermute(gt[:, p * width : (p + 1) * width], axis, [(i, i ^ p) for i in range(n)])
        total = total + got.astype(jnp.float32)
    return total.T


def pair_index(index, me, per_run):
    return (me ^ (index // per_run)) * per_run + index % per_run


def rotate_index(index, me, n, per_run):
    run = index // per_run
    return ((me - run) % n) * per_run + index % per_run


def body(emb_in, ctx_in, pos_weight, neg_weight, tile_row, tile_col, tile_count):
    n_row = lax.axis_size("row")
    n_col = lax.axis_size("col")
    me_row = lax.axis_index("row")
    me_col = lax.axis_index("col")
    pos = pos_weight[0, 0]
    neg = neg_weight[0, 0]
    tile = pos.shape[-1]
    per_run = emb_in.shape[0] // tile
    rows = rotate_index(tile_row[0, 0], me_col, n_col, per_run)
    if paired(n_row):
        cols = pair_index(tile_col[0, 0], me_row, per_run)
        gathers = (gather_paired, gather_xor)
        scatters = (scatter_xor_t, scatter_paired_t)
    else:
        cols = rotate_index(tile_col[0, 0], me_row, n_row, per_run)
        gathers = (gather_rotated, gather_rotated)
        scatters = (scatter_rotated_t, scatter_rotated_t)
    count = tile_count[0, 0]
    emb = emb_in
    ctx = ctx_in
    for iteration in range(ITERS):
        emb_low = gather_rotated(emb.astype(jnp.bfloat16), "col", n_col)
        first, last = iteration == 0, iteration == ITERS - 1
        ctx_low = gathers[0 if first else 1](ctx.astype(jnp.bfloat16), "row", n_row)
        grad_emb, grad_ctx_t = tile_sweep(pos, neg, rows, cols, count, emb_low, ctx_low)
        emb = emb + 0.05 * scatter_rotated(grad_emb, "col", n_col)
        ctx = ctx + 0.05 * scatters[1 if last else 0](grad_ctx_t, "row", n_row)
    return (emb, ctx)


def solution(mesh):
    in_specs = (
        P(("row", "col"), None),
        P(("row", "col"), None),
        P("row", "col", None, None, None),
        P("row", "col", None, None, None),
        P("row", "col", None),
        P("row", "col", None),
        P("row", "col"),
    )
    out_specs = (P(("row", "col"), None), P(("row", "col"), None))
    return jax.shard_map(body, mesh=mesh, in_specs=in_specs, out_specs=out_specs, check_vma=False)
```

```python
import functools

import jax
import jax.numpy as jnp
from jax import lax
from jax.experimental import pallas as pl
from jax.experimental.pallas import tpu as pltpu
from jax.sharding import PartitionSpec as P

ITERS = 2


def sweep_kernel(tile, group, rows_ref, cols_ref, count_ref, emb_ref, ctx_ref, pos_ref, neg_ref,
                 gemb_ref, gctx_ref, acc_e, acc_c):
    k = pl.program_id(0)
    n = count_ref[0]

    @pl.when(k == 0)
    def _():
        acc_e[...] = jnp.zeros_like(acc_e)
        acc_c[...] = jnp.zeros_like(acc_c)

    def visit(j):
        slot = k * group + j
        r0 = pl.multiple_of(rows_ref[slot] * tile, tile)
        c0 = pl.multiple_of(cols_ref[slot] * tile, tile)
        e = emb_ref[pl.ds(r0, tile), :]
        c = ctx_ref[pl.ds(c0, tile), :]
        score = lax.dot_general(e, c, (((1,), (1,)), ((), ())), preferred_element_type=jnp.float32)
        positive = pos_ref[j].astype(jnp.float32)
        negative = neg_ref[j].astype(jnp.float32)
        t = jnp.tanh(score * 0.5)
        coeff = (0.5 * ((positive - negative) - (positive + negative) * t)).astype(jnp.bfloat16)
        acc_e[pl.ds(r0, tile), :] += jnp.dot(coeff, c, preferred_element_type=jnp.float32)
        acc_c[pl.ds(c0, tile), :] += lax.dot_general(
            coeff, e, (((0,), (0,)), ((), ())), preferred_element_type=jnp.float32
        )

    full = (k + 1) * group <= n

    @pl.when(full)
    def _():
        for j in range(group):
            visit(j)

    @pl.when(jnp.logical_not(full))
    def _():
        for j in range(group):
            pl.when(k * group + j < n)(functools.partial(visit, j))

    @pl.when(k == pl.num_programs(0) - 1)
    def _():
        gemb_ref[...] = acc_e[...].astype(gemb_ref.dtype)
        gctx_ref[...] = acc_c[...].astype(gctx_ref.dtype)


def tile_sweep(pos, neg, rows, cols, count, emb_low, ctx_low):
    cap, tile, _ = pos.shape
    ne, dim = emb_low.shape
    nc = ctx_low.shape[0]
    group = next(g for g in (8, 4, 2, 1) if cap % g == 0)

    def slot(k, rows_ref, cols_ref, count_ref):
        last = jnp.maximum((count_ref[0] + group - 1) // group - 1, 0)
        return (jnp.minimum(k, last), 0, 0)

    grid_spec = pltpu.PrefetchScalarGridSpec(
        num_scalar_prefetch=3,
        grid=(cap // group,),
        in_specs=[
            pl.BlockSpec((ne, dim), lambda k, *_: (0, 0)),
            pl.BlockSpec((nc, dim), lambda k, *_: (0, 0)),
            pl.BlockSpec((group, tile, tile), slot),
            pl.BlockSpec((group, tile, tile), slot),
        ],
        out_specs=[
            pl.BlockSpec((ne, dim), lambda k, *_: (0, 0)),
            pl.BlockSpec((nc, dim), lambda k, *_: (0, 0)),
        ],
        scratch_shapes=[
            pltpu.VMEM((ne, dim), jnp.float32),
            pltpu.VMEM((nc, dim), jnp.float32),
        ],
    )
    flops = cap * 3 * 2 * tile * tile * dim
    return pl.pallas_call(
        functools.partial(sweep_kernel, tile, group),
        grid_spec=grid_spec,
        out_shape=(
            jax.ShapeDtypeStruct((ne, dim), jnp.bfloat16),
            jax.ShapeDtypeStruct((nc, dim), jnp.bfloat16),
        ),
        compiler_params=pltpu.CompilerParams(dimension_semantics=("arbitrary",)),
        cost_estimate=pl.CostEstimate(
            flops=flops,
            transcendentals=cap * tile * tile,
            bytes_accessed=2 * cap * tile * tile * 2 + 3 * (ne + nc) * dim * 2,
        ),
    )(rows, cols, count.reshape(1), emb_low, ctx_low, pos, neg)


def gather_rotated(x, axis, n):
    pieces = [x]
    for s in range(1, n):
        pieces.append(lax.ppermute(x, axis, [(i, (i + s) % n) for i in range(n)]))
    return jnp.concatenate(pieces, axis=0)


def scatter_rotated(g, axis, n):
    chunks = g.reshape(n, -1, g.shape[-1])
    total = chunks[0].astype(jnp.float32)
    for s in range(1, n):
        got = lax.ppermute(chunks[(n - s) % n], axis, [(i, (i + s) % n) for i in range(n)])
        total = total + got.astype(jnp.float32)
    return total


def paired(n):
    return n % 2 == 0 and n & (n - 1) == 0


def gather_paired(x, axis, n):
    pair = jnp.concatenate([x, lax.ppermute(x, axis, [(i, i ^ 1) for i in range(n)])], axis=0)
    blocks = [pair]
    for b in range(1, n // 2):
        blocks.append(lax.ppermute(pair, axis, [(i, i ^ (2 * b)) for i in range(n)]))
    return jnp.concatenate(blocks, axis=0)


def scatter_paired(g, axis, n):
    width = g.shape[0] // n
    total = g[: 2 * width].astype(jnp.float32)
    for b in range(1, n // 2):
        got = lax.ppermute(g[2 * b * width : (2 * b + 2) * width], axis, [(i, i ^ (2 * b)) for i in range(n)])
        total = total + got.astype(jnp.float32)
    got = lax.ppermute(total[width:], axis, [(i, i ^ 1) for i in range(n)])
    return total[:width] + got


def gather_xor(x, axis, n):
    pieces = [x]
    for p in range(1, n):
        pieces.append(lax.ppermute(x, axis, [(i, i ^ p) for i in range(n)]))
    return jnp.concatenate(pieces, axis=0)


def scatter_xor(g, axis, n):
    width = g.shape[0] // n
    total = g[:width].astype(jnp.float32)
    for p in range(1, n):
        got = lax.ppermute(g[p * width : (p + 1) * width], axis, [(i, i ^ p) for i in range(n)])
        total = total + got.astype(jnp.float32)
    return total


def pair_index(index, me, per_run):
    return (me ^ (index // per_run)) * per_run + index % per_run


def rotate_index(index, me, n, per_run):
    run = index // per_run
    return ((me - run) % n) * per_run + index % per_run


def body(emb_in, ctx_in, pos_weight, neg_weight, tile_row, tile_col, tile_count):
    n_row = lax.axis_size("row")
    n_col = lax.axis_size("col")
    me_row = lax.axis_index("row")
    me_col = lax.axis_index("col")
    pos = pos_weight[0, 0]
    neg = neg_weight[0, 0]
    tile = pos.shape[-1]
    per_run = emb_in.shape[0] // tile
    rows = rotate_index(tile_row[0, 0], me_col, n_col, per_run)
    if paired(n_row):
        cols = pair_index(tile_col[0, 0], me_row, per_run)
        gathers = (gather_paired, gather_xor)
        scatters = (scatter_xor, scatter_paired)
    else:
        cols = rotate_index(tile_col[0, 0], me_row, n_row, per_run)
        gathers = (gather_rotated, gather_rotated)
        scatters = (scatter_rotated, scatter_rotated)
    count = tile_count[0, 0]
    emb = emb_in
    ctx = ctx_in
    for iteration in range(ITERS):
        emb_low = gather_rotated(emb.astype(jnp.bfloat16), "col", n_col)
        first, last = iteration == 0, iteration == ITERS - 1
        ctx_low = gathers[0 if first else 1](ctx.astype(jnp.bfloat16), "row", n_row)
        grad_emb, grad_ctx = tile_sweep(pos, neg, rows, cols, count, emb_low, ctx_low)
        emb = emb + 0.05 * scatter_rotated(grad_emb, "col", n_col)
        ctx = ctx + 0.05 * scatters[1 if last else 0](grad_ctx, "row", n_row)
    return (emb, ctx)


def solution(mesh):
    in_specs = (
        P(("row", "col"), None),
        P(("row", "col"), None),
        P("row", "col", None, None, None),
        P("row", "col", None, None, None),
        P("row", "col", None),
        P("row", "col", None),
        P("row", "col"),
    )
    out_specs = (P(("row", "col"), None), P(("row", "col"), None))
    return jax.shard_map(body, mesh=mesh, in_specs=in_specs, out_specs=out_specs, check_vma=False)
```

```python
import functools

import jax
import jax.numpy as jnp
from jax import lax
from jax.experimental import pallas as pl
from jax.experimental.pallas import tpu as pltpu
from jax.sharding import PartitionSpec as P

ITERS = 2


def sweep_kernel(tile, group, rows_ref, cols_ref, count_ref, emb_ref, ctx_ref, pos_ref, neg_ref,
                 gemb_ref, gctx_ref, acc_e, acc_ct, emb_t):
    k = pl.program_id(0)
    n = count_ref[0]

    @pl.when(k == 0)
    def _():
        acc_e[...] = jnp.zeros_like(acc_e)
        acc_ct[...] = jnp.zeros_like(acc_ct)
        emb_t[...] = emb_ref[...].astype(jnp.float32).T.astype(emb_t.dtype)

    def visit(j):
        slot = k * group + j
        r0 = pl.multiple_of(rows_ref[slot] * tile, tile)
        c0 = pl.multiple_of(cols_ref[slot] * tile, tile)
        e = emb_ref[pl.ds(r0, tile), :]
        c = ctx_ref[pl.ds(c0, tile), :]
        score = lax.dot_general(e, c, (((1,), (1,)), ((), ())), preferred_element_type=jnp.float32)
        positive = pos_ref[j].astype(jnp.float32)
        negative = neg_ref[j].astype(jnp.float32)
        t = jnp.tanh(score * 0.5)
        coeff = (0.5 * ((positive - negative) - (positive + negative) * t)).astype(jnp.bfloat16)
        acc_e[pl.ds(r0, tile), :] += jnp.dot(coeff, c, preferred_element_type=jnp.float32)
        acc_ct[:, pl.ds(c0, tile)] += jnp.dot(
            emb_t[:, pl.ds(r0, tile)], coeff, preferred_element_type=jnp.float32
        )

    full = (k + 1) * group <= n

    @pl.when(full)
    def _():
        for j in range(group):
            visit(j)

    @pl.when(jnp.logical_not(full))
    def _():
        for j in range(group):
            pl.when(k * group + j < n)(functools.partial(visit, j))

    @pl.when(k == pl.num_programs(0) - 1)
    def _():
        gemb_ref[...] = acc_e[...].astype(gemb_ref.dtype)
        gctx_ref[...] = acc_ct[...].T.astype(gctx_ref.dtype)


def tile_sweep(pos, neg, rows, cols, count, emb_low, ctx_low):
    cap, tile, _ = pos.shape
    ne, dim = emb_low.shape
    nc = ctx_low.shape[0]
    group = next(g for g in (8, 4, 2, 1) if cap % g == 0)

    def slot(k, rows_ref, cols_ref, count_ref):
        last = jnp.maximum((count_ref[0] + group - 1) // group - 1, 0)
        return (jnp.minimum(k, last), 0, 0)

    grid_spec = pltpu.PrefetchScalarGridSpec(
        num_scalar_prefetch=3,
        grid=(cap // group,),
        in_specs=[
            pl.BlockSpec((ne, dim), lambda k, *_: (0, 0)),
            pl.BlockSpec((nc, dim), lambda k, *_: (0, 0)),
            pl.BlockSpec((group, tile, tile), slot),
            pl.BlockSpec((group, tile, tile), slot),
        ],
        out_specs=[
            pl.BlockSpec((ne, dim), lambda k, *_: (0, 0)),
            pl.BlockSpec((nc, dim), lambda k, *_: (0, 0)),
        ],
        scratch_shapes=[
            pltpu.VMEM((ne, dim), jnp.float32),
            pltpu.VMEM((dim, nc), jnp.float32),
            pltpu.VMEM((dim, ne), jnp.bfloat16),
        ],
    )
    flops = cap * 3 * 2 * tile * tile * dim
    return pl.pallas_call(
        functools.partial(sweep_kernel, tile, group),
        grid_spec=grid_spec,
        out_shape=(
            jax.ShapeDtypeStruct((ne, dim), jnp.bfloat16),
            jax.ShapeDtypeStruct((nc, dim), jnp.bfloat16),
        ),
        compiler_params=pltpu.CompilerParams(dimension_semantics=("arbitrary",)),
        cost_estimate=pl.CostEstimate(
            flops=flops,
            transcendentals=cap * tile * tile,
            bytes_accessed=2 * cap * tile * tile * 2 + 3 * (ne + nc) * dim * 2,
        ),
    )(rows, cols, count.reshape(1), emb_low, ctx_low, pos, neg)


def gather_rotated(x, axis, n):
    pieces = [x]
    for s in range(1, n):
        pieces.append(lax.ppermute(x, axis, [(i, (i + s) % n) for i in range(n)]))
    return jnp.concatenate(pieces, axis=0)


def scatter_rotated(g, axis, n):
    chunks = g.reshape(n, -1, g.shape[-1])
    total = chunks[0].astype(jnp.float32)
    for s in range(1, n):
        got = lax.ppermute(chunks[(n - s) % n], axis, [(i, (i + s) % n) for i in range(n)])
        total = total + got.astype(jnp.float32)
    return total


def paired(n):
    return n % 2 == 0 and n & (n - 1) == 0


def gather_paired(x, axis, n):
    pair = jnp.concatenate([x, lax.ppermute(x, axis, [(i, i ^ 1) for i in range(n)])], axis=0)
    blocks = [pair]
    for b in range(1, n // 2):
        blocks.append(lax.ppermute(pair, axis, [(i, i ^ (2 * b)) for i in range(n)]))
    return jnp.concatenate(blocks, axis=0)


def scatter_paired(g, axis, n):
    width = g.shape[0] // n
    total = g[: 2 * width].astype(jnp.float32)
    for b in range(1, n // 2):
        got = lax.ppermute(g[2 * b * width : (2 * b + 2) * width], axis, [(i, i ^ (2 * b)) for i in range(n)])
        total = total + got.astype(jnp.float32)
    got = lax.ppermute(total[width:], axis, [(i, i ^ 1) for i in range(n)])
    return total[:width] + got


def gather_xor(x, axis, n):
    pieces = [x]
    for p in range(1, n):
        pieces.append(lax.ppermute(x, axis, [(i, i ^ p) for i in range(n)]))
    return jnp.concatenate(pieces, axis=0)


def scatter_xor(g, axis, n):
    width = g.shape[0] // n
    total = g[:width].astype(jnp.float32)
    for p in range(1, n):
        got = lax.ppermute(g[p * width : (p + 1) * width], axis, [(i, i ^ p) for i in range(n)])
        total = total + got.astype(jnp.float32)
    return total


def pair_index(index, me, per_run):
    return (me ^ (index // per_run)) * per_run + index % per_run


def rotate_index(index, me, n, per_run):
    run = index // per_run
    return ((me - run) % n) * per_run + index % per_run


def body(emb_in, ctx_in, pos_weight, neg_weight, tile_row, tile_col, tile_count):
    n_row = lax.axis_size("row")
    n_col = lax.axis_size("col")
    me_row = lax.axis_index("row")
    me_col = lax.axis_index("col")
    pos = pos_weight[0, 0]
    neg = neg_weight[0, 0]
    tile = pos.shape[-1]
    per_run = emb_in.shape[0] // tile
    rows = rotate_index(tile_row[0, 0], me_col, n_col, per_run)
    if paired(n_row):
        cols = pair_index(tile_col[0, 0], me_row, per_run)
        gathers = (gather_paired, gather_xor)
        scatters = (scatter_xor, scatter_paired)
    else:
        cols = rotate_index(tile_col[0, 0], me_row, n_row, per_run)
        gathers = (gather_rotated, gather_rotated)
        scatters = (scatter_rotated, scatter_rotated)
    count = tile_count[0, 0]
    emb = emb_in
    ctx = ctx_in
    for iteration in range(ITERS):
        emb_low = gather_rotated(emb.astype(jnp.bfloat16), "col", n_col)
        first, last = iteration == 0, iteration == ITERS - 1
        ctx_low = gathers[0 if first else 1](ctx.astype(jnp.bfloat16), "row", n_row)
        grad_emb, grad_ctx = tile_sweep(pos, neg, rows, cols, count, emb_low, ctx_low)
        emb = emb + 0.05 * scatter_rotated(grad_emb, "col", n_col)
        ctx = ctx + 0.05 * scatters[1 if last else 0](grad_ctx, "row", n_row)
    return (emb, ctx)


def solution(mesh):
    in_specs = (
        P(("row", "col"), None),
        P(("row", "col"), None),
        P("row", "col", None, None, None),
        P("row", "col", None, None, None),
        P("row", "col", None),
        P("row", "col", None),
        P("row", "col"),
    )
    out_specs = (P(("row", "col"), None), P(("row", "col"), None))
    return jax.shard_map(body, mesh=mesh, in_specs=in_specs, out_specs=out_specs, check_vma=False)
```

```python
import functools

import jax
import jax.numpy as jnp
from jax import lax
from jax.experimental import pallas as pl
from jax.experimental.pallas import tpu as pltpu
from jax.sharding import PartitionSpec as P

ITERS = 2


def sweep_kernel(tile, group, rows_ref, cols_ref, count_ref, emb_ref, ctx_ref, pos_ref, neg_ref,
                 gemb_ref, gctx_ref, acc_e, acc_ct, emb_t):
    k = pl.program_id(0)
    n = count_ref[0]

    @pl.when(k == 0)
    def _():
        acc_e[...] = jnp.zeros_like(acc_e)
        acc_ct[...] = jnp.zeros_like(acc_ct)
        emb_t[...] = emb_ref[...].astype(jnp.float32).T.astype(emb_t.dtype)

    def visit(j):
        slot = k * group + j
        r0 = pl.multiple_of(rows_ref[slot] * tile, tile)
        c0 = pl.multiple_of(cols_ref[slot] * tile, tile)
        e = emb_ref[pl.ds(r0, tile), :]
        c = ctx_ref[pl.ds(c0, tile), :]
        score = lax.dot_general(e, c, (((1,), (1,)), ((), ())), preferred_element_type=jnp.float32)
        positive = pos_ref[j].astype(jnp.float32)
        negative = neg_ref[j].astype(jnp.float32)
        t = jnp.tanh(score * 0.5)
        coeff = (0.5 * ((positive - negative) - (positive + negative) * t)).astype(jnp.bfloat16)
        acc_e[pl.ds(r0, tile), :] += jnp.dot(coeff, c, preferred_element_type=jnp.float32)
        acc_ct[:, pl.ds(c0, tile)] += jnp.dot(
            emb_t[:, pl.ds(r0, tile)], coeff, preferred_element_type=jnp.float32
        )

    full = (k + 1) * group <= n

    @pl.when(full)
    def _():
        for j in range(group):
            visit(j)

    @pl.when(jnp.logical_not(full))
    def _():
        for j in range(group):
            pl.when(k * group + j < n)(functools.partial(visit, j))

    @pl.when(k == pl.num_programs(0) - 1)
    def _():
        gemb_ref[...] = acc_e[...].astype(gemb_ref.dtype)
        gctx_ref[...] = acc_ct[...].T.astype(gctx_ref.dtype)


def tile_sweep(pos, neg, rows, cols, count, emb_low, ctx_low):
    cap, tile, _ = pos.shape
    ne, dim = emb_low.shape
    nc = ctx_low.shape[0]
    group = next(g for g in (8, 4, 2, 1) if cap % g == 0)

    def slot(k, rows_ref, cols_ref, count_ref):
        last = jnp.maximum((count_ref[0] + group - 1) // group - 1, 0)
        return (jnp.minimum(k, last), 0, 0)

    grid_spec = pltpu.PrefetchScalarGridSpec(
        num_scalar_prefetch=3,
        grid=(cap // group,),
        in_specs=[
            pl.BlockSpec((ne, dim), lambda k, *_: (0, 0)),
            pl.BlockSpec((nc, dim), lambda k, *_: (0, 0)),
            pl.BlockSpec((group, tile, tile), slot),
            pl.BlockSpec((group, tile, tile), slot),
        ],
        out_specs=[
            pl.BlockSpec((ne, dim), lambda k, *_: (0, 0)),
            pl.BlockSpec((nc, dim), lambda k, *_: (0, 0)),
        ],
        scratch_shapes=[
            pltpu.VMEM((ne, dim), jnp.float32),
            pltpu.VMEM((dim, nc), jnp.float32),
            pltpu.VMEM((dim, ne), jnp.bfloat16),
        ],
    )
    flops = cap * 3 * 2 * tile * tile * dim
    return pl.pallas_call(
        functools.partial(sweep_kernel, tile, group),
        grid_spec=grid_spec,
        out_shape=(
            jax.ShapeDtypeStruct((ne, dim), jnp.bfloat16),
            jax.ShapeDtypeStruct((nc, dim), jnp.bfloat16),
        ),
        compiler_params=pltpu.CompilerParams(dimension_semantics=("arbitrary",)),
        cost_estimate=pl.CostEstimate(
            flops=flops,
            transcendentals=cap * tile * tile,
            bytes_accessed=2 * cap * tile * tile * 2 + 3 * (ne + nc) * dim * 2,
        ),
    )(rows, cols, count.reshape(1), emb_low, ctx_low, pos, neg)


def gather_rotated(x, axis, n):
    pieces = [x]
    for s in range(1, n):
        pieces.append(lax.ppermute(x, axis, [(i, (i + s) % n) for i in range(n)]))
    return jnp.concatenate(pieces, axis=0)


def scatter_rotated(g, axis, n):
    chunks = g.reshape(n, -1, g.shape[-1])
    total = chunks[0].astype(jnp.float32)
    for s in range(1, n):
        got = lax.ppermute(chunks[(n - s) % n], axis, [(i, (i + s) % n) for i in range(n)])
        total = total + got.astype(jnp.float32)
    return total


def paired(n):
    return n % 2 == 0 and n & (n - 1) == 0


def gather_paired(x, axis, n):
    pair = jnp.concatenate([x, lax.ppermute(x, axis, [(i, i ^ 1) for i in range(n)])], axis=0)
    blocks = [pair]
    for b in range(1, n // 2):
        blocks.append(lax.ppermute(pair, axis, [(i, i ^ (2 * b)) for i in range(n)]))
    return jnp.concatenate(blocks, axis=0)


def scatter_paired(g, axis, n):
    width = g.shape[0] // n
    total = g[: 2 * width].astype(jnp.float32)
    for b in range(1, n // 2):
        got = lax.ppermute(g[2 * b * width : (2 * b + 2) * width], axis, [(i, i ^ (2 * b)) for i in range(n)])
        total = total + got.astype(jnp.float32)
    got = lax.ppermute(total[width:], axis, [(i, i ^ 1) for i in range(n)])
    return total[:width] + got


def spread_pairs(pair, axis, n):
    blocks = [pair]
    for b in range(1, n // 2):
        blocks.append(lax.ppermute(pair, axis, [(i, i ^ (2 * b)) for i in range(n)]))
    return jnp.concatenate(blocks, axis=0)


def reduce_pairs(g, axis, n):
    width = g.shape[0] // n
    total = g[: 2 * width].astype(jnp.float32)
    for b in range(1, n // 2):
        got = lax.ppermute(g[2 * b * width : (2 * b + 2) * width], axis, [(i, i ^ (2 * b)) for i in range(n)])
        total = total + got.astype(jnp.float32)
    other = lax.ppermute(total, axis, [(i, i ^ 1) for i in range(n)])
    return total + jnp.concatenate([other[width:], other[:width]], axis=0)


def gather_xor(x, axis, n):
    pieces = [x]
    for p in range(1, n):
        pieces.append(lax.ppermute(x, axis, [(i, i ^ p) for i in range(n)]))
    return jnp.concatenate(pieces, axis=0)


def scatter_xor(g, axis, n):
    width = g.shape[0] // n
    total = g[:width].astype(jnp.float32)
    for p in range(1, n):
        got = lax.ppermute(g[p * width : (p + 1) * width], axis, [(i, i ^ p) for i in range(n)])
        total = total + got.astype(jnp.float32)
    return total


def pair_index(index, me, per_run):
    return (me ^ (index // per_run)) * per_run + index % per_run


def rotate_index(index, me, n, per_run):
    run = index // per_run
    return ((me - run) % n) * per_run + index % per_run


def body(emb_in, ctx_in, pos_weight, neg_weight, tile_row, tile_col, tile_count):
    n_row = lax.axis_size("row")
    n_col = lax.axis_size("col")
    me_row = lax.axis_index("row")
    me_col = lax.axis_index("col")
    pos = pos_weight[0, 0]
    neg = neg_weight[0, 0]
    tile = pos.shape[-1]
    per_run = emb_in.shape[0] // tile
    rows = rotate_index(tile_row[0, 0], me_col, n_col, per_run)
    if paired(n_row):
        cols = pair_index(tile_col[0, 0], me_row, per_run)
        gathers = (gather_paired, gather_xor)
        scatters = (scatter_xor, scatter_paired)
    else:
        cols = rotate_index(tile_col[0, 0], me_row, n_row, per_run)
        gathers = (gather_rotated, gather_rotated)
        scatters = (scatter_rotated, scatter_rotated)
    count = tile_count[0, 0]
    width = ctx_in.shape[0]
    emb = emb_in
    ctx = ctx_in
    pair = None
    for iteration in range(ITERS):
        first, last = iteration == 0, iteration == ITERS - 1
        emb_low = gather_rotated(emb.astype(jnp.bfloat16), "col", n_col)
        if not paired(n_row):
            ctx_low = gathers[0](ctx.astype(jnp.bfloat16), "row", n_row)
        else:
            if first:
                partner = lax.ppermute(ctx, "row", [(i, i ^ 1) for i in range(n_row)])
                pair = jnp.concatenate([ctx, partner], axis=0)
            ctx_low = spread_pairs(pair.astype(jnp.bfloat16), "row", n_row)
        grad_emb, grad_ctx = tile_sweep(pos, neg, rows, cols, count, emb_low, ctx_low)
        emb = emb + 0.05 * scatter_rotated(grad_emb, "col", n_col)
        if not paired(n_row):
            ctx = ctx + 0.05 * scatters[0](grad_ctx, "row", n_row)
        elif last:
            ctx = pair[:width] + 0.05 * scatter_paired(grad_ctx, "row", n_row)
        else:
            pair = pair + 0.05 * reduce_pairs(grad_ctx, "row", n_row)
    return (emb, ctx)


def solution(mesh):
    in_specs = (
        P(("row", "col"), None),
        P(("row", "col"), None),
        P("row", "col", None, None, None),
        P("row", "col", None, None, None),
        P("row", "col", None),
        P("row", "col", None),
        P("row", "col"),
    )
    out_specs = (P(("row", "col"), None), P(("row", "col"), None))
    return jax.shard_map(body, mesh=mesh, in_specs=in_specs, out_specs=out_specs, check_vma=False)
```

```python
import functools

import jax
import jax.numpy as jnp
from jax import lax
from jax.experimental import pallas as pl
from jax.experimental.pallas import tpu as pltpu
from jax.sharding import PartitionSpec as P

ITERS = 2


def sweep_kernel(tile, group, n_emb, n_ctx, rows_ref, cols_ref, count_ref, *refs):
    emb_pieces = refs[:n_emb]
    ctx_pieces = refs[n_emb : n_emb + n_ctx]
    pos_ref, neg_ref, gemb_ref, gctx_ref, acc_e, acc_ct, emb_t, emb_ref, ctx_ref = refs[n_emb + n_ctx :]
    k = pl.program_id(0)
    n = count_ref[0]

    @pl.when(k == 0)
    def _():
        at = 0
        for piece in emb_pieces:
            rows = piece.shape[0]
            emb_ref[at : at + rows, :] = piece[...]
            emb_t[:, at : at + rows] = piece[...].astype(jnp.float32).T.astype(emb_t.dtype)
            at += rows
        at = 0
        for piece in ctx_pieces:
            rows = piece.shape[0]
            ctx_ref[at : at + rows, :] = piece[...]
            at += rows
        acc_e[...] = jnp.zeros_like(acc_e)
        acc_ct[...] = jnp.zeros_like(acc_ct)

    def visit(j):
        slot = k * group + j
        r0 = pl.multiple_of(rows_ref[slot] * tile, tile)
        c0 = pl.multiple_of(cols_ref[slot] * tile, tile)
        e = emb_ref[pl.ds(r0, tile), :]
        c = ctx_ref[pl.ds(c0, tile), :]
        score = lax.dot_general(e, c, (((1,), (1,)), ((), ())), preferred_element_type=jnp.float32)
        positive = pos_ref[j].astype(jnp.float32)
        negative = neg_ref[j].astype(jnp.float32)
        t = jnp.tanh(score * 0.5)
        coeff = (0.5 * ((positive - negative) - (positive + negative) * t)).astype(jnp.bfloat16)
        acc_e[pl.ds(r0, tile), :] += jnp.dot(coeff, c, preferred_element_type=jnp.float32)
        acc_ct[:, pl.ds(c0, tile)] += jnp.dot(
            emb_t[:, pl.ds(r0, tile)], coeff, preferred_element_type=jnp.float32
        )

    full = (k + 1) * group <= n

    @pl.when(full)
    def _():
        for j in range(group):
            visit(j)

    @pl.when(jnp.logical_not(full))
    def _():
        for j in range(group):
            pl.when(k * group + j < n)(functools.partial(visit, j))

    @pl.when(k == pl.num_programs(0) - 1)
    def _():
        gemb_ref[...] = acc_e[...].astype(gemb_ref.dtype)
        gctx_ref[...] = acc_ct[...].T.astype(gctx_ref.dtype)


def tile_sweep(pos, neg, rows, cols, count, emb_pieces, ctx_pieces):
    cap, tile, _ = pos.shape
    dim = emb_pieces[0].shape[1]
    ne = sum(p.shape[0] for p in emb_pieces)
    nc = sum(p.shape[0] for p in ctx_pieces)
    group = next(g for g in (8, 4, 2, 1) if cap % g == 0)

    def slot(k, rows_ref, cols_ref, count_ref):
        last = jnp.maximum((count_ref[0] + group - 1) // group - 1, 0)
        return (jnp.minimum(k, last), 0, 0)

    grid_spec = pltpu.PrefetchScalarGridSpec(
        num_scalar_prefetch=3,
        grid=(cap // group,),
        in_specs=[pl.BlockSpec(p.shape, lambda k, *_: (0, 0)) for p in emb_pieces + ctx_pieces]
        + [
            pl.BlockSpec((group, tile, tile), slot),
            pl.BlockSpec((group, tile, tile), slot),
        ],
        out_specs=[
            pl.BlockSpec((ne, dim), lambda k, *_: (0, 0)),
            pl.BlockSpec((nc, dim), lambda k, *_: (0, 0)),
        ],
        scratch_shapes=[
            pltpu.VMEM((ne, dim), jnp.float32),
            pltpu.VMEM((dim, nc), jnp.float32),
            pltpu.VMEM((dim, ne), jnp.bfloat16),
            pltpu.VMEM((ne, dim), jnp.bfloat16),
            pltpu.VMEM((nc, dim), jnp.bfloat16),
        ],
    )
    flops = cap * 3 * 2 * tile * tile * dim
    return pl.pallas_call(
        functools.partial(sweep_kernel, tile, group, len(emb_pieces), len(ctx_pieces)),
        grid_spec=grid_spec,
        out_shape=(
            jax.ShapeDtypeStruct((ne, dim), jnp.bfloat16),
            jax.ShapeDtypeStruct((nc, dim), jnp.bfloat16),
        ),
        compiler_params=pltpu.CompilerParams(dimension_semantics=("arbitrary",)),
        cost_estimate=pl.CostEstimate(
            flops=flops,
            transcendentals=cap * tile * tile,
            bytes_accessed=2 * cap * tile * tile * 2 + 3 * (ne + nc) * dim * 2,
        ),
    )(rows, cols, count.reshape(1), *emb_pieces, *ctx_pieces, pos, neg)


def gather_rotated(x, axis, n):
    pieces = [x]
    for s in range(1, n):
        pieces.append(lax.ppermute(x, axis, [(i, (i + s) % n) for i in range(n)]))
    return pieces


def scatter_rotated(g, axis, n):
    chunks = g.reshape(n, -1, g.shape[-1])
    total = chunks[0].astype(jnp.float32)
    for s in range(1, n):
        got = lax.ppermute(chunks[(n - s) % n], axis, [(i, (i + s) % n) for i in range(n)])
        total = total + got.astype(jnp.float32)
    return total


def paired(n):
    return n % 2 == 0 and n & (n - 1) == 0


def gather_paired(x, axis, n):
    pair = jnp.concatenate([x, lax.ppermute(x, axis, [(i, i ^ 1) for i in range(n)])], axis=0)
    blocks = [pair]
    for b in range(1, n // 2):
        blocks.append(lax.ppermute(pair, axis, [(i, i ^ (2 * b)) for i in range(n)]))
    return blocks


def scatter_paired(g, axis, n):
    width = g.shape[0] // n
    total = g[: 2 * width].astype(jnp.float32)
    for b in range(1, n // 2):
        got = lax.ppermute(g[2 * b * width : (2 * b + 2) * width], axis, [(i, i ^ (2 * b)) for i in range(n)])
        total = total + got.astype(jnp.float32)
    got = lax.ppermute(total[width:], axis, [(i, i ^ 1) for i in range(n)])
    return total[:width] + got


def gather_xor(x, axis, n):
    pieces = [x]
    for p in range(1, n):
        pieces.append(lax.ppermute(x, axis, [(i, i ^ p) for i in range(n)]))
    return pieces


def scatter_xor(g, axis, n):
    width = g.shape[0] // n
    total = g[:width].astype(jnp.float32)
    for p in range(1, n):
        got = lax.ppermute(g[p * width : (p + 1) * width], axis, [(i, i ^ p) for i in range(n)])
        total = total + got.astype(jnp.float32)
    return total


def pair_index(index, me, per_run):
    return (me ^ (index // per_run)) * per_run + index % per_run


def rotate_index(index, me, n, per_run):
    run = index // per_run
    return ((me - run) % n) * per_run + index % per_run


def body(emb_in, ctx_in, pos_weight, neg_weight, tile_row, tile_col, tile_count):
    n_row = lax.axis_size("row")
    n_col = lax.axis_size("col")
    me_row = lax.axis_index("row")
    me_col = lax.axis_index("col")
    pos = pos_weight[0, 0]
    neg = neg_weight[0, 0]
    tile = pos.shape[-1]
    per_run = emb_in.shape[0] // tile
    rows = rotate_index(tile_row[0, 0], me_col, n_col, per_run)
    if paired(n_row):
        cols = pair_index(tile_col[0, 0], me_row, per_run)
        gathers = (gather_paired, gather_xor)
        scatters = (scatter_xor, scatter_paired)
    else:
        cols = rotate_index(tile_col[0, 0], me_row, n_row, per_run)
        gathers = (gather_rotated, gather_rotated)
        scatters = (scatter_rotated, scatter_rotated)
    count = tile_count[0, 0]
    emb = emb_in
    ctx = ctx_in
    for iteration in range(ITERS):
        emb_low = gather_rotated(emb.astype(jnp.bfloat16), "col", n_col)
        first, last = iteration == 0, iteration == ITERS - 1
        ctx_low = gathers[0 if first else 1](ctx.astype(jnp.bfloat16), "row", n_row)
        grad_emb, grad_ctx = tile_sweep(pos, neg, rows, cols, count, emb_low, ctx_low)
        emb = emb + 0.05 * scatter_rotated(grad_emb, "col", n_col)
        ctx = ctx + 0.05 * scatters[1 if last else 0](grad_ctx, "row", n_row)
    return (emb, ctx)


def solution(mesh):
    in_specs = (
        P(("row", "col"), None),
        P(("row", "col"), None),
        P("row", "col", None, None, None),
        P("row", "col", None, None, None),
        P("row", "col", None),
        P("row", "col", None),
        P("row", "col"),
    )
    out_specs = (P(("row", "col"), None), P(("row", "col"), None))
    return jax.shard_map(body, mesh=mesh, in_specs=in_specs, out_specs=out_specs, check_vma=False)
```

```python
import functools

import jax
import jax.numpy as jnp
from jax import lax
from jax.experimental import pallas as pl
from jax.experimental.pallas import tpu as pltpu
from jax.sharding import PartitionSpec as P

ITERS = 2


def sweep_kernel(tile, group, n_emb, n_ctx, n_gemb, n_gctx, rows_ref, cols_ref, count_ref, *refs):
    emb_pieces = refs[:n_emb]
    ctx_pieces = refs[n_emb : n_emb + n_ctx]
    pos_ref, neg_ref = refs[n_emb + n_ctx : n_emb + n_ctx + 2]
    outs = refs[n_emb + n_ctx + 2 : n_emb + n_ctx + 2 + n_gemb + n_gctx]
    gemb_refs, gctx_refs = outs[:n_gemb], outs[n_gemb:]
    acc_e, acc_ct, emb_t, emb_ref, ctx_ref = refs[n_emb + n_ctx + 2 + n_gemb + n_gctx :]
    k = pl.program_id(0)
    n = count_ref[0]

    @pl.when(k == 0)
    def _():
        at = 0
        for piece in emb_pieces:
            rows = piece.shape[0]
            emb_ref[at : at + rows, :] = piece[...]
            emb_t[:, at : at + rows] = piece[...].astype(jnp.float32).T.astype(emb_t.dtype)
            at += rows
        at = 0
        for piece in ctx_pieces:
            rows = piece.shape[0]
            ctx_ref[at : at + rows, :] = piece[...]
            at += rows
        acc_e[...] = jnp.zeros_like(acc_e)
        acc_ct[...] = jnp.zeros_like(acc_ct)

    def visit(j):
        slot = k * group + j
        r0 = pl.multiple_of(rows_ref[slot] * tile, tile)
        c0 = pl.multiple_of(cols_ref[slot] * tile, tile)
        e = emb_ref[pl.ds(r0, tile), :]
        c = ctx_ref[pl.ds(c0, tile), :]
        score = lax.dot_general(e, c, (((1,), (1,)), ((), ())), preferred_element_type=jnp.float32)
        positive = pos_ref[j].astype(jnp.float32)
        negative = neg_ref[j].astype(jnp.float32)
        t = jnp.tanh(score * 0.5)
        coeff = (0.5 * ((positive - negative) - (positive + negative) * t)).astype(jnp.bfloat16)
        acc_e[pl.ds(r0, tile), :] += jnp.dot(coeff, c, preferred_element_type=jnp.float32)
        acc_ct[:, pl.ds(c0, tile)] += jnp.dot(
            emb_t[:, pl.ds(r0, tile)], coeff, preferred_element_type=jnp.float32
        )

    full = (k + 1) * group <= n

    @pl.when(full)
    def _():
        for j in range(group):
            visit(j)

    @pl.when(jnp.logical_not(full))
    def _():
        for j in range(group):
            pl.when(k * group + j < n)(functools.partial(visit, j))

    @pl.when(k == pl.num_programs(0) - 1)
    def _():
        for p, out in enumerate(gemb_refs):
            rows = out.shape[0]
            out[...] = acc_e[p * rows : (p + 1) * rows, :].astype(out.dtype)
        for p, out in enumerate(gctx_refs):
            rows = out.shape[0]
            out[...] = acc_ct[:, p * rows : (p + 1) * rows].T.astype(out.dtype)


def tile_sweep(pos, neg, rows, cols, count, emb_pieces, ctx_pieces, n_gemb, n_gctx):
    cap, tile, _ = pos.shape
    dim = emb_pieces[0].shape[1]
    ne = sum(p.shape[0] for p in emb_pieces)
    nc = sum(p.shape[0] for p in ctx_pieces)
    group = next(g for g in (8, 4, 2, 1) if cap % g == 0)

    def slot(k, rows_ref, cols_ref, count_ref):
        last = jnp.maximum((count_ref[0] + group - 1) // group - 1, 0)
        return (jnp.minimum(k, last), 0, 0)

    grid_spec = pltpu.PrefetchScalarGridSpec(
        num_scalar_prefetch=3,
        grid=(cap // group,),
        in_specs=[pl.BlockSpec(p.shape, lambda k, *_: (0, 0)) for p in emb_pieces + ctx_pieces]
        + [
            pl.BlockSpec((group, tile, tile), slot),
            pl.BlockSpec((group, tile, tile), slot),
        ],
        out_specs=[pl.BlockSpec((ne // n_gemb, dim), lambda k, *_: (0, 0))] * n_gemb
        + [pl.BlockSpec((nc // n_gctx, dim), lambda k, *_: (0, 0))] * n_gctx,
        scratch_shapes=[
            pltpu.VMEM((ne, dim), jnp.float32),
            pltpu.VMEM((dim, nc), jnp.float32),
            pltpu.VMEM((dim, ne), jnp.bfloat16),
            pltpu.VMEM((ne, dim), jnp.bfloat16),
            pltpu.VMEM((nc, dim), jnp.bfloat16),
        ],
    )
    flops = cap * 3 * 2 * tile * tile * dim
    outs = pl.pallas_call(
        functools.partial(sweep_kernel, tile, group, len(emb_pieces), len(ctx_pieces), n_gemb, n_gctx),
        grid_spec=grid_spec,
        out_shape=[jax.ShapeDtypeStruct((ne // n_gemb, dim), jnp.bfloat16)] * n_gemb
        + [jax.ShapeDtypeStruct((nc // n_gctx, dim), jnp.bfloat16)] * n_gctx,
        compiler_params=pltpu.CompilerParams(dimension_semantics=("arbitrary",)),
        cost_estimate=pl.CostEstimate(
            flops=flops,
            transcendentals=cap * tile * tile,
            bytes_accessed=2 * cap * tile * tile * 2 + 3 * (ne + nc) * dim * 2,
        ),
    )(rows, cols, count.reshape(1), *emb_pieces, *ctx_pieces, pos, neg)
    return outs[:n_gemb], outs[n_gemb:]


def gather_rotated(x, axis, n):
    pieces = [x]
    for s in range(1, n):
        pieces.append(lax.ppermute(x, axis, [(i, (i + s) % n) for i in range(n)]))
    return pieces


def scatter_rotated(chunks, axis, n):
    total = chunks[0].astype(jnp.float32)
    for s in range(1, n):
        got = lax.ppermute(chunks[(n - s) % n], axis, [(i, (i + s) % n) for i in range(n)])
        total = total + got.astype(jnp.float32)
    return total


def paired(n):
    return n % 2 == 0 and n & (n - 1) == 0


def gather_paired(x, axis, n):
    pair = jnp.concatenate([x, lax.ppermute(x, axis, [(i, i ^ 1) for i in range(n)])], axis=0)
    blocks = [pair]
    for b in range(1, n // 2):
        blocks.append(lax.ppermute(pair, axis, [(i, i ^ (2 * b)) for i in range(n)]))
    return blocks


def scatter_paired(blocks, axis, n):
    total = blocks[0].astype(jnp.float32)
    for b in range(1, n // 2):
        got = lax.ppermute(blocks[b], axis, [(i, i ^ (2 * b)) for i in range(n)])
        total = total + got.astype(jnp.float32)
    width = total.shape[0] // 2
    got = lax.ppermute(total[width:], axis, [(i, i ^ 1) for i in range(n)])
    return total[:width] + got


def gather_xor(x, axis, n):
    pieces = [x]
    for p in range(1, n):
        pieces.append(lax.ppermute(x, axis, [(i, i ^ p) for i in range(n)]))
    return pieces


def scatter_xor(chunks, axis, n):
    total = chunks[0].astype(jnp.float32)
    for p in range(1, n):
        got = lax.ppermute(chunks[p], axis, [(i, i ^ p) for i in range(n)])
        total = total + got.astype(jnp.float32)
    return total


def pair_index(index, me, per_run):
    return (me ^ (index // per_run)) * per_run + index % per_run


def rotate_index(index, me, n, per_run):
    run = index // per_run
    return ((me - run) % n) * per_run + index % per_run


def body(emb_in, ctx_in, pos_weight, neg_weight, tile_row, tile_col, tile_count):
    n_row = lax.axis_size("row")
    n_col = lax.axis_size("col")
    me_row = lax.axis_index("row")
    me_col = lax.axis_index("col")
    pos = pos_weight[0, 0]
    neg = neg_weight[0, 0]
    tile = pos.shape[-1]
    per_run = emb_in.shape[0] // tile
    rows = rotate_index(tile_row[0, 0], me_col, n_col, per_run)
    if paired(n_row):
        cols = pair_index(tile_col[0, 0], me_row, per_run)
        gathers = (gather_paired, gather_xor)
        scatters = (scatter_xor, scatter_paired)
        splits = (n_row, n_row // 2)
    else:
        cols = rotate_index(tile_col[0, 0], me_row, n_row, per_run)
        gathers = (gather_rotated, gather_rotated)
        scatters = (scatter_rotated, scatter_rotated)
        splits = (n_row, n_row)
    count = tile_count[0, 0]
    emb = emb_in
    ctx = ctx_in
    for iteration in range(ITERS):
        emb_low = gather_rotated(emb.astype(jnp.bfloat16), "col", n_col)
        first, last = iteration == 0, iteration == ITERS - 1
        ctx_low = gathers[0 if first else 1](ctx.astype(jnp.bfloat16), "row", n_row)
        grad_emb, grad_ctx = tile_sweep(
            pos, neg, rows, cols, count, emb_low, ctx_low, n_col, splits[1 if last else 0]
        )
        emb = emb + 0.05 * scatter_rotated(grad_emb, "col", n_col)
        ctx = ctx + 0.05 * scatters[1 if last else 0](grad_ctx, "row", n_row)
    return (emb, ctx)


def solution(mesh):
    in_specs = (
        P(("row", "col"), None),
        P(("row", "col"), None),
        P("row", "col", None, None, None),
        P("row", "col", None, None, None),
        P("row", "col", None),
        P("row", "col", None),
        P("row", "col"),
    )
    out_specs = (P(("row", "col"), None), P(("row", "col"), None))
    return jax.shard_map(body, mesh=mesh, in_specs=in_specs, out_specs=out_specs, check_vma=False)
```

```python
import functools

import jax
import jax.numpy as jnp
from jax import lax
from jax.experimental import pallas as pl
from jax.experimental.pallas import tpu as pltpu
from jax.sharding import PartitionSpec as P

ITERS = 2


def sweep_kernel(tile, group, n_emb, n_ctx, n_gemb, n_gctx, rows_ref, cols_ref, count_ref, *refs):
    emb_pieces = refs[:n_emb]
    ctx_pieces = refs[n_emb : n_emb + n_ctx]
    pos_ref, neg_ref = refs[n_emb + n_ctx : n_emb + n_ctx + 2]
    outs = refs[n_emb + n_ctx + 2 : n_emb + n_ctx + 2 + n_gemb + n_gctx]
    gemb_refs, gctx_refs = outs[:n_gemb], outs[n_gemb:]
    acc_e, acc_ct, emb_t, emb_ref, ctx_ref = refs[n_emb + n_ctx + 2 + n_gemb + n_gctx :]
    k = pl.program_id(0)
    n = count_ref[0]

    @pl.when(k == 0)
    def _():
        at = 0
        for piece in emb_pieces:
            rows = piece.shape[0]
            emb_ref[at : at + rows, :] = piece[...]
            emb_t[:, at : at + rows] = piece[...].astype(jnp.float32).T.astype(emb_t.dtype)
            at += rows
        at = 0
        for piece in ctx_pieces:
            rows = piece.shape[0]
            ctx_ref[at : at + rows, :] = piece[...]
            at += rows
        acc_e[...] = jnp.zeros_like(acc_e)
        acc_ct[...] = jnp.zeros_like(acc_ct)

    def visit(j):
        slot = k * group + j
        r0 = pl.multiple_of(rows_ref[slot] * tile, tile)
        c0 = pl.multiple_of(cols_ref[slot] * tile, tile)
        e = emb_ref[pl.ds(r0, tile), :]
        c = ctx_ref[pl.ds(c0, tile), :]
        score = lax.dot_general(e, c, (((1,), (1,)), ((), ())), preferred_element_type=jnp.float32)
        positive = pos_ref[j].astype(jnp.float32)
        negative = neg_ref[j].astype(jnp.float32)
        t = jnp.tanh(score * 0.5)
        coeff = (0.5 * ((positive - negative) - (positive + negative) * t)).astype(jnp.bfloat16)
        acc_e[pl.ds(r0, tile), :] += jnp.dot(coeff, c, preferred_element_type=jnp.float32)
        acc_ct[:, pl.ds(c0, tile)] += jnp.dot(
            emb_t[:, pl.ds(r0, tile)], coeff, preferred_element_type=jnp.float32
        )

    full = (k + 1) * group <= n

    @pl.when(full)
    def _():
        for j in range(group):
            visit(j)

    @pl.when(jnp.logical_not(full))
    def _():
        for j in range(group):
            pl.when(k * group + j < n)(functools.partial(visit, j))

    @pl.when(k == pl.num_programs(0) - 1)
    def _():
        for p, out in enumerate(gemb_refs):
            rows = out.shape[0]
            out[...] = acc_e[p * rows : (p + 1) * rows, :].astype(out.dtype)
        for p, out in enumerate(gctx_refs):
            rows = out.shape[0]
            out[...] = acc_ct[:, p * rows : (p + 1) * rows].T.astype(out.dtype)


def tile_sweep(pos, neg, rows, cols, count, emb_pieces, ctx_pieces, n_gemb, n_gctx):
    cap, tile, _ = pos.shape
    dim = emb_pieces[0].shape[1]
    ne = sum(p.shape[0] for p in emb_pieces)
    nc = sum(p.shape[0] for p in ctx_pieces)
    group = next(g for g in (8, 4, 2, 1) if cap % g == 0)

    def slot(k, rows_ref, cols_ref, count_ref):
        last = jnp.maximum((count_ref[0] + group - 1) // group - 1, 0)
        return (jnp.minimum(k, last), 0, 0)

    grid_spec = pltpu.PrefetchScalarGridSpec(
        num_scalar_prefetch=3,
        grid=(cap // group,),
        in_specs=[pl.BlockSpec(p.shape, lambda k, *_: (0, 0)) for p in emb_pieces + ctx_pieces]
        + [
            pl.BlockSpec((group, tile, tile), slot),
            pl.BlockSpec((group, tile, tile), slot),
        ],
        out_specs=[pl.BlockSpec((ne // n_gemb, dim), lambda k, *_: (0, 0))] * n_gemb
        + [pl.BlockSpec((nc // n_gctx, dim), lambda k, *_: (0, 0))] * n_gctx,
        scratch_shapes=[
            pltpu.VMEM((ne, dim), jnp.float32),
            pltpu.VMEM((dim, nc), jnp.float32),
            pltpu.VMEM((dim, ne), jnp.bfloat16),
            pltpu.VMEM((ne, dim), jnp.bfloat16),
            pltpu.VMEM((nc, dim), jnp.bfloat16),
        ],
    )
    flops = cap * 3 * 2 * tile * tile * dim
    outs = pl.pallas_call(
        functools.partial(sweep_kernel, tile, group, len(emb_pieces), len(ctx_pieces), n_gemb, n_gctx),
        grid_spec=grid_spec,
        out_shape=[jax.ShapeDtypeStruct((ne // n_gemb, dim), jnp.bfloat16)] * n_gemb
        + [jax.ShapeDtypeStruct((nc // n_gctx, dim), jnp.bfloat16)] * n_gctx,
        compiler_params=pltpu.CompilerParams(dimension_semantics=("arbitrary",)),
        cost_estimate=pl.CostEstimate(
            flops=flops,
            transcendentals=cap * tile * tile,
            bytes_accessed=2 * cap * tile * tile * 2 + 3 * (ne + nc) * dim * 2,
        ),
    )(rows, cols, count.reshape(1), *emb_pieces, *ctx_pieces, pos, neg)
    return outs[:n_gemb], outs[n_gemb:]


def gather_rotated(x, axis, n):
    pieces = [x]
    for s in range(1, n):
        pieces.append(lax.ppermute(x, axis, [(i, (i + s) % n) for i in range(n)]))
    return pieces


def scatter_rotated(chunks, axis, n):
    total = chunks[0].astype(jnp.float32)
    for s in range(1, n):
        got = lax.ppermute(chunks[(n - s) % n], axis, [(i, (i + s) % n) for i in range(n)])
        total = total + got.astype(jnp.float32)
    return total


def paired(n):
    return n % 2 == 0 and n & (n - 1) == 0


def gather_paired(x, axis, n):
    pair = jnp.concatenate([x, lax.ppermute(x, axis, [(i, i ^ 1) for i in range(n)])], axis=0)
    blocks = [pair]
    for b in range(1, n // 2):
        blocks.append(lax.ppermute(pair, axis, [(i, i ^ (2 * b)) for i in range(n)]))
    return blocks


def scatter_paired(blocks, axis, n):
    total = blocks[0].astype(jnp.float32)
    for b in range(1, n // 2):
        got = lax.ppermute(blocks[b], axis, [(i, i ^ (2 * b)) for i in range(n)])
        total = total + got.astype(jnp.float32)
    width = total.shape[0] // 2
    got = lax.ppermute(total[width:], axis, [(i, i ^ 1) for i in range(n)])
    return total[:width] + got


def gather_xor(x, axis, n):
    pieces = [x]
    for p in range(1, n):
        pieces.append(lax.ppermute(x, axis, [(i, i ^ p) for i in range(n)]))
    return pieces


def scatter_xor(chunks, axis, n):
    total = chunks[0].astype(jnp.float32)
    for p in range(1, n):
        got = lax.ppermute(chunks[p], axis, [(i, i ^ p) for i in range(n)])
        total = total + got.astype(jnp.float32)
    return total


def pair_index(index, me, per_run):
    return (me ^ (index // per_run)) * per_run + index % per_run


def rotate_index(index, me, n, per_run):
    run = index // per_run
    return ((me - run) % n) * per_run + index % per_run


def plan(index, me, n, per_run):
    if paired(n):
        return pair_index(index, me, per_run), (
            (gather_paired, gather_xor),
            (scatter_xor, scatter_paired),
            (n, n // 2),
        )
    return rotate_index(index, me, n, per_run), (
        (gather_rotated, gather_rotated),
        (scatter_rotated, scatter_rotated),
        (n, n),
    )


def body(emb_in, ctx_in, pos_weight, neg_weight, tile_row, tile_col, tile_count):
    n_row = lax.axis_size("row")
    n_col = lax.axis_size("col")
    me_row = lax.axis_index("row")
    me_col = lax.axis_index("col")
    pos = pos_weight[0, 0]
    neg = neg_weight[0, 0]
    tile = pos.shape[-1]
    per_run = emb_in.shape[0] // tile
    rows, emb_plan = plan(tile_row[0, 0], me_col, n_col, per_run)
    cols, ctx_plan = plan(tile_col[0, 0], me_row, n_row, per_run)
    count = tile_count[0, 0]
    emb = emb_in
    ctx = ctx_in
    for iteration in range(ITERS):
        first, last = iteration == 0, iteration == ITERS - 1
        emb_low = emb_plan[0][0 if first else 1](emb.astype(jnp.bfloat16), "col", n_col)
        ctx_low = ctx_plan[0][0 if first else 1](ctx.astype(jnp.bfloat16), "row", n_row)
        grad_emb, grad_ctx = tile_sweep(
            pos, neg, rows, cols, count, emb_low, ctx_low,
            emb_plan[2][1 if last else 0], ctx_plan[2][1 if last else 0],
        )
        emb = emb + 0.05 * emb_plan[1][1 if last else 0](grad_emb, "col", n_col)
        ctx = ctx + 0.05 * ctx_plan[1][1 if last else 0](grad_ctx, "row", n_row)
    return (emb, ctx)


def solution(mesh):
    in_specs = (
        P(("row", "col"), None),
        P(("row", "col"), None),
        P("row", "col", None, None, None),
        P("row", "col", None, None, None),
        P("row", "col", None),
        P("row", "col", None),
        P("row", "col"),
    )
    out_specs = (P(("row", "col"), None), P(("row", "col"), None))
    return jax.shard_map(body, mesh=mesh, in_specs=in_specs, out_specs=out_specs, check_vma=False)
```

```python
import functools

import jax
import jax.numpy as jnp
from jax import lax
from jax.experimental import pallas as pl
from jax.experimental.pallas import tpu as pltpu
from jax.sharding import PartitionSpec as P

ITERS = 2


def sweep_kernel(tile, group, n_emb, n_ctx, n_gemb, n_gctx, rows_ref, cols_ref, count_ref, *refs):
    emb_pieces = refs[:n_emb]
    ctx_pieces = refs[n_emb : n_emb + n_ctx]
    pos_ref, neg_ref = refs[n_emb + n_ctx : n_emb + n_ctx + 2]
    outs = refs[n_emb + n_ctx + 2 : n_emb + n_ctx + 2 + n_gemb + n_gctx]
    gemb_refs, gctx_refs = outs[:n_gemb], outs[n_gemb:]
    acc_e, acc_ct, emb_t, emb_ref, ctx_ref = refs[n_emb + n_ctx + 2 + n_gemb + n_gctx :]
    k = pl.program_id(0)
    n = count_ref[0]

    @pl.when(k == 0)
    def _():
        at = 0
        for piece in emb_pieces:
            rows = piece.shape[0]
            emb_ref[at : at + rows, :] = piece[...]
            emb_t[:, at : at + rows] = piece[...].astype(jnp.float32).T.astype(emb_t.dtype)
            at += rows
        at = 0
        for piece in ctx_pieces:
            rows = piece.shape[0]
            ctx_ref[at : at + rows, :] = piece[...]
            at += rows
        acc_e[...] = jnp.zeros_like(acc_e)
        acc_ct[...] = jnp.zeros_like(acc_ct)

    def visit(j):
        slot = k * group + j
        r0 = pl.multiple_of(rows_ref[slot] * tile, tile)
        c0 = pl.multiple_of(cols_ref[slot] * tile, tile)
        e = emb_ref[pl.ds(r0, tile), :]
        c = ctx_ref[pl.ds(c0, tile), :]
        score = lax.dot_general(e, c, (((1,), (1,)), ((), ())), preferred_element_type=jnp.float32)
        positive = pos_ref[j].astype(jnp.float32)
        negative = neg_ref[j].astype(jnp.float32)
        t = jnp.tanh(score * 0.5)
        coeff = (0.5 * ((positive - negative) - (positive + negative) * t)).astype(jnp.bfloat16)
        acc_e[pl.ds(r0, tile), :] += jnp.dot(coeff, c, preferred_element_type=jnp.float32)
        acc_ct[:, pl.ds(c0, tile)] += jnp.dot(
            emb_t[:, pl.ds(r0, tile)], coeff, preferred_element_type=jnp.float32
        )

    full = (k + 1) * group <= n

    @pl.when(full)
    def _():
        for j in range(group):
            visit(j)

    @pl.when(jnp.logical_not(full))
    def _():
        for j in range(group):
            pl.when(k * group + j < n)(functools.partial(visit, j))

    @pl.when(k == pl.num_programs(0) - 1)
    def _():
        for p, out in enumerate(gemb_refs):
            rows = out.shape[0]
            out[...] = acc_e[p * rows : (p + 1) * rows, :].astype(out.dtype)
        for p, out in enumerate(gctx_refs):
            rows = out.shape[0]
            out[...] = acc_ct[:, p * rows : (p + 1) * rows].T.astype(out.dtype)


def tile_sweep(pos, neg, rows, cols, count, emb_pieces, ctx_pieces, n_gemb, n_gctx):
    cap, tile, _ = pos.shape
    dim = emb_pieces[0].shape[1]
    ne = sum(p.shape[0] for p in emb_pieces)
    nc = sum(p.shape[0] for p in ctx_pieces)
    group = next(g for g in (8, 4, 2, 1) if cap % g == 0)

    def slot(k, rows_ref, cols_ref, count_ref):
        last = jnp.maximum((count_ref[0] + group - 1) // group - 1, 0)
        return (jnp.minimum(k, last), 0, 0)

    grid_spec = pltpu.PrefetchScalarGridSpec(
        num_scalar_prefetch=3,
        grid=(cap // group,),
        in_specs=[pl.BlockSpec(p.shape, lambda k, *_: (0, 0)) for p in emb_pieces + ctx_pieces]
        + [
            pl.BlockSpec((group, tile, tile), slot),
            pl.BlockSpec((group, tile, tile), slot),
        ],
        out_specs=[pl.BlockSpec((ne // n_gemb, dim), lambda k, *_: (0, 0))] * n_gemb
        + [pl.BlockSpec((nc // n_gctx, dim), lambda k, *_: (0, 0))] * n_gctx,
        scratch_shapes=[
            pltpu.VMEM((ne, dim), jnp.float32),
            pltpu.VMEM((dim, nc), jnp.float32),
            pltpu.VMEM((dim, ne), jnp.bfloat16),
            pltpu.VMEM((ne, dim), jnp.bfloat16),
            pltpu.VMEM((nc, dim), jnp.bfloat16),
        ],
    )
    flops = cap * 3 * 2 * tile * tile * dim
    outs = pl.pallas_call(
        functools.partial(sweep_kernel, tile, group, len(emb_pieces), len(ctx_pieces), n_gemb, n_gctx),
        grid_spec=grid_spec,
        out_shape=[jax.ShapeDtypeStruct((ne // n_gemb, dim), jnp.bfloat16)] * n_gemb
        + [jax.ShapeDtypeStruct((nc // n_gctx, dim), jnp.bfloat16)] * n_gctx,
        compiler_params=pltpu.CompilerParams(dimension_semantics=("arbitrary",)),
        cost_estimate=pl.CostEstimate(
            flops=flops,
            transcendentals=cap * tile * tile,
            bytes_accessed=2 * cap * tile * tile * 2 + 3 * (ne + nc) * dim * 2,
        ),
    )(rows, cols, count.reshape(1), *emb_pieces, *ctx_pieces, pos, neg)
    return outs[:n_gemb], outs[n_gemb:]


def gather_rotated(x, axis, n):
    pieces = [x]
    for s in range(1, n):
        pieces.append(lax.ppermute(x, axis, [(i, (i + s) % n) for i in range(n)]))
    return pieces


def scatter_rotated(chunks, axis, n):
    total = chunks[0].astype(jnp.float32)
    for s in range(1, n):
        got = lax.ppermute(chunks[(n - s) % n], axis, [(i, (i + s) % n) for i in range(n)])
        total = total + got.astype(jnp.float32)
    return total


def paired(n):
    return n % 2 == 0 and n & (n - 1) == 0


def gather_paired(x, axis, n):
    pair = jnp.concatenate([x, lax.ppermute(x, axis, [(i, i ^ 1) for i in range(n)])], axis=0)
    blocks = [pair]
    for b in range(1, n // 2):
        blocks.append(lax.ppermute(pair, axis, [(i, i ^ (2 * b)) for i in range(n)]))
    return blocks


def scatter_paired(blocks, axis, n):
    total = blocks[0].astype(jnp.float32)
    for b in range(1, n // 2):
        got = lax.ppermute(blocks[b], axis, [(i, i ^ (2 * b)) for i in range(n)])
        total = total + got.astype(jnp.float32)
    width = total.shape[0] // 2
    got = lax.ppermute(total[width:], axis, [(i, i ^ 1) for i in range(n)])
    return total[:width] + got


def gather_xor(x, axis, n):
    pieces = [x]
    for p in range(1, n):
        pieces.append(lax.ppermute(x, axis, [(i, i ^ p) for i in range(n)]))
    return pieces


def scatter_xor(chunks, axis, n):
    total = chunks[0].astype(jnp.float32)
    for p in range(1, n):
        got = lax.ppermute(chunks[p], axis, [(i, i ^ p) for i in range(n)])
        total = total + got.astype(jnp.float32)
    return total


def pair_index(index, me, per_run):
    return (me ^ (index // per_run)) * per_run + index % per_run


def rotate_index(index, me, n, per_run):
    run = index // per_run
    return ((me - run) % n) * per_run + index % per_run


def body(emb_in, ctx_in, pos_weight, neg_weight, tile_row, tile_col, tile_count):
    n_row = lax.axis_size("row")
    n_col = lax.axis_size("col")
    me_row = lax.axis_index("row")
    me_col = lax.axis_index("col")
    pos = pos_weight[0, 0]
    neg = neg_weight[0, 0]
    tile = pos.shape[-1]
    per_run = emb_in.shape[0] // tile
    rows = rotate_index(tile_row[0, 0], me_col, n_col, per_run)
    if paired(n_row):
        cols = pair_index(tile_col[0, 0], me_row, per_run)
        gathers = (gather_paired, gather_xor)
        scatters = (scatter_paired, scatter_paired)
        splits = (n_row // 2, n_row // 2)
    else:
        cols = rotate_index(tile_col[0, 0], me_row, n_row, per_run)
        gathers = (gather_rotated, gather_rotated)
        scatters = (scatter_rotated, scatter_rotated)
        splits = (n_row, n_row)
    count = tile_count[0, 0]
    emb = emb_in
    ctx = ctx_in
    for iteration in range(ITERS):
        emb_low = gather_rotated(emb.astype(jnp.bfloat16), "col", n_col)
        first, last = iteration == 0, iteration == ITERS - 1
        ctx_low = gathers[0 if first else 1](ctx.astype(jnp.bfloat16), "row", n_row)
        grad_emb, grad_ctx = tile_sweep(
            pos, neg, rows, cols, count, emb_low, ctx_low, n_col, splits[1 if last else 0]
        )
        emb = emb + 0.05 * scatter_rotated(grad_emb, "col", n_col)
        ctx = ctx + 0.05 * scatters[1 if last else 0](grad_ctx, "row", n_row)
    return (emb, ctx)


def solution(mesh):
    in_specs = (
        P(("row", "col"), None),
        P(("row", "col"), None),
        P("row", "col", None, None, None),
        P("row", "col", None, None, None),
        P("row", "col", None),
        P("row", "col", None),
        P("row", "col"),
    )
    out_specs = (P(("row", "col"), None), P(("row", "col"), None))
    return jax.shard_map(body, mesh=mesh, in_specs=in_specs, out_specs=out_specs, check_vma=False)
```

```python
import functools

import jax
import jax.numpy as jnp
from jax import lax
from jax.experimental import pallas as pl
from jax.experimental.pallas import tpu as pltpu
from jax.sharding import PartitionSpec as P

ITERS = 2


def sweep_kernel(tile, group, n_emb, n_ctx, n_gemb, n_gctx, rows_ref, cols_ref, count_ref, *refs):
    emb_pieces = refs[:n_emb]
    ctx_pieces = refs[n_emb : n_emb + n_ctx]
    pos_ref, neg_ref = refs[n_emb + n_ctx : n_emb + n_ctx + 2]
    outs = refs[n_emb + n_ctx + 2 : n_emb + n_ctx + 2 + n_gemb + n_gctx]
    gemb_refs, gctx_refs = outs[:n_gemb], outs[n_gemb:]
    acc_e, acc_ct, emb_t, emb_ref, ctx_ref = refs[n_emb + n_ctx + 2 + n_gemb + n_gctx :]
    k = pl.program_id(0)
    n = count_ref[0]

    @pl.when(k == 0)
    def _():
        at = 0
        for piece in emb_pieces:
            rows = piece.shape[0]
            emb_ref[at : at + rows, :] = piece[...]
            emb_t[:, at : at + rows] = piece[...].astype(jnp.float32).T.astype(emb_t.dtype)
            at += rows
        at = 0
        for piece in ctx_pieces:
            rows = piece.shape[0]
            ctx_ref[at : at + rows, :] = piece[...]
            at += rows
        acc_e[...] = jnp.zeros_like(acc_e)
        acc_ct[...] = jnp.zeros_like(acc_ct)

    def visit(j):
        slot = k * group + j
        r0 = pl.multiple_of(rows_ref[slot] * tile, tile)
        c0 = pl.multiple_of(cols_ref[slot] * tile, tile)
        e = emb_ref[pl.ds(r0, tile), :]
        c = ctx_ref[pl.ds(c0, tile), :]
        score = lax.dot_general(e, c, (((1,), (1,)), ((), ())), preferred_element_type=jnp.float32)
        positive = pos_ref[j].astype(jnp.float32)
        negative = neg_ref[j].astype(jnp.float32)
        t = jnp.tanh(score * 0.5)
        coeff = (0.5 * ((positive - negative) - (positive + negative) * t)).astype(jnp.bfloat16)
        acc_e[pl.ds(r0, tile), :] += jnp.dot(coeff, c, preferred_element_type=jnp.float32)
        acc_ct[:, pl.ds(c0, tile)] += jnp.dot(
            emb_t[:, pl.ds(r0, tile)], coeff, preferred_element_type=jnp.float32
        )

    full = (k + 1) * group <= n

    @pl.when(full)
    def _():
        for j in range(group):
            visit(j)

    @pl.when(jnp.logical_not(full))
    def _():
        for j in range(group):
            pl.when(k * group + j < n)(functools.partial(visit, j))

    @pl.when(k == pl.num_programs(0) - 1)
    def _():
        for p, out in enumerate(gemb_refs):
            rows = out.shape[0]
            out[...] = acc_e[p * rows : (p + 1) * rows, :].astype(out.dtype)
        for p, out in enumerate(gctx_refs):
            rows = out.shape[0]
            out[...] = acc_ct[:, p * rows : (p + 1) * rows].T.astype(out.dtype)


def tile_sweep(pos, neg, rows, cols, count, emb_pieces, ctx_pieces, n_gemb, n_gctx):
    cap, tile, _ = pos.shape
    dim = emb_pieces[0].shape[1]
    ne = sum(p.shape[0] for p in emb_pieces)
    nc = sum(p.shape[0] for p in ctx_pieces)
    group = next(g for g in (8, 4, 2, 1) if cap % g == 0)

    def slot(k, rows_ref, cols_ref, count_ref):
        last = jnp.maximum((count_ref[0] + group - 1) // group - 1, 0)
        return (jnp.minimum(k, last), 0, 0)

    grid_spec = pltpu.PrefetchScalarGridSpec(
        num_scalar_prefetch=3,
        grid=(cap // group,),
        in_specs=[pl.BlockSpec(p.shape, lambda k, *_: (0, 0)) for p in emb_pieces + ctx_pieces]
        + [
            pl.BlockSpec((group, tile, tile), slot),
            pl.BlockSpec((group, tile, tile), slot),
        ],
        out_specs=[pl.BlockSpec((ne // n_gemb, dim), lambda k, *_: (0, 0))] * n_gemb
        + [pl.BlockSpec((nc // n_gctx, dim), lambda k, *_: (0, 0))] * n_gctx,
        scratch_shapes=[
            pltpu.VMEM((ne, dim), jnp.float32),
            pltpu.VMEM((dim, nc), jnp.float32),
            pltpu.VMEM((dim, ne), jnp.bfloat16),
            pltpu.VMEM((ne, dim), jnp.bfloat16),
            pltpu.VMEM((nc, dim), jnp.bfloat16),
        ],
    )
    flops = cap * 3 * 2 * tile * tile * dim
    outs = pl.pallas_call(
        functools.partial(sweep_kernel, tile, group, len(emb_pieces), len(ctx_pieces), n_gemb, n_gctx),
        grid_spec=grid_spec,
        out_shape=[jax.ShapeDtypeStruct((ne // n_gemb, dim), jnp.bfloat16)] * n_gemb
        + [jax.ShapeDtypeStruct((nc // n_gctx, dim), jnp.bfloat16)] * n_gctx,
        compiler_params=pltpu.CompilerParams(dimension_semantics=("arbitrary",)),
        cost_estimate=pl.CostEstimate(
            flops=flops,
            transcendentals=cap * tile * tile,
            bytes_accessed=2 * cap * tile * tile * 2 + 3 * (ne + nc) * dim * 2,
        ),
    )(rows, cols, count.reshape(1), *emb_pieces, *ctx_pieces, pos, neg)
    return outs[:n_gemb], outs[n_gemb:]


def gather_rotated(x, axis, n):
    pieces = [x]
    for s in range(1, n):
        pieces.append(lax.ppermute(x, axis, [(i, (i + s) % n) for i in range(n)]))
    return pieces


def scatter_rotated(chunks, axis, n):
    total = chunks[0].astype(jnp.float32)
    for s in range(1, n):
        got = lax.ppermute(chunks[(n - s) % n], axis, [(i, (i + s) % n) for i in range(n)])
        total = total + got.astype(jnp.float32)
    return total


def paired(n):
    return n % 2 == 0 and n & (n - 1) == 0


def gather_paired(x, axis, n):
    pair = jnp.concatenate([x, lax.ppermute(x, axis, [(i, i ^ 1) for i in range(n)])], axis=0)
    blocks = [pair]
    for b in range(1, n // 2):
        blocks.append(lax.ppermute(pair, axis, [(i, i ^ (2 * b)) for i in range(n)]))
    return blocks


def scatter_paired(blocks, axis, n):
    total = blocks[0].astype(jnp.float32)
    for b in range(1, n // 2):
        got = lax.ppermute(blocks[b], axis, [(i, i ^ (2 * b)) for i in range(n)])
        total = total + got.astype(jnp.float32)
    width = total.shape[0] // 2
    got = lax.ppermute(total[width:], axis, [(i, i ^ 1) for i in range(n)])
    return total[:width] + got


def gather_xor(x, axis, n):
    pieces = [x]
    for p in range(1, n):
        pieces.append(lax.ppermute(x, axis, [(i, i ^ p) for i in range(n)]))
    return pieces


def scatter_xor(chunks, axis, n):
    total = chunks[0].astype(jnp.float32)
    for p in range(1, n):
        got = lax.ppermute(chunks[p], axis, [(i, i ^ p) for i in range(n)])
        total = total + got.astype(jnp.float32)
    return total


def pair_index(index, me, per_run):
    return (me ^ (index // per_run)) * per_run + index % per_run


def rotate_index(index, me, n, per_run):
    run = index // per_run
    return ((me - run) % n) * per_run + index % per_run


def body(emb_in, ctx_in, pos_weight, neg_weight, tile_row, tile_col, tile_count):
    n_row = lax.axis_size("row")
    n_col = lax.axis_size("col")
    me_row = lax.axis_index("row")
    me_col = lax.axis_index("col")
    pos = pos_weight[0, 0]
    neg = neg_weight[0, 0]
    tile = pos.shape[-1]
    per_run = emb_in.shape[0] // tile
    rows = rotate_index(tile_row[0, 0], me_col, n_col, per_run)
    if paired(n_row):
        cols = pair_index(tile_col[0, 0], me_row, per_run)
        gathers = (gather_paired, gather_paired)
        scatters = (scatter_paired, scatter_paired)
        splits = (n_row // 2, n_row // 2)
    else:
        cols = rotate_index(tile_col[0, 0], me_row, n_row, per_run)
        gathers = (gather_rotated, gather_rotated)
        scatters = (scatter_rotated, scatter_rotated)
        splits = (n_row, n_row)
    count = tile_count[0, 0]
    emb = emb_in
    ctx = ctx_in
    for iteration in range(ITERS):
        emb_low = gather_rotated(emb.astype(jnp.bfloat16), "col", n_col)
        first, last = iteration == 0, iteration == ITERS - 1
        ctx_low = gathers[0 if first else 1](ctx.astype(jnp.bfloat16), "row", n_row)
        grad_emb, grad_ctx = tile_sweep(
            pos, neg, rows, cols, count, emb_low, ctx_low, n_col, splits[1 if last else 0]
        )
        emb = emb + 0.05 * scatter_rotated(grad_emb, "col", n_col)
        ctx = ctx + 0.05 * scatters[1 if last else 0](grad_ctx, "row", n_row)
    return (emb, ctx)


def solution(mesh):
    in_specs = (
        P(("row", "col"), None),
        P(("row", "col"), None),
        P("row", "col", None, None, None),
        P("row", "col", None, None, None),
        P("row", "col", None),
        P("row", "col", None),
        P("row", "col"),
    )
    out_specs = (P(("row", "col"), None), P(("row", "col"), None))
    return jax.shard_map(body, mesh=mesh, in_specs=in_specs, out_specs=out_specs, check_vma=False)
```

```python
import functools

import jax
import jax.numpy as jnp
from jax import lax
from jax.experimental import pallas as pl
from jax.experimental.pallas import tpu as pltpu
from jax.sharding import PartitionSpec as P

ITERS = 2


def sweep_kernel(tile, group, n_emb, n_ctx, n_gemb, n_gctx, rows_ref, cols_ref, count_ref, *refs):
    emb_pieces = refs[:n_emb]
    ctx_pieces = refs[n_emb : n_emb + n_ctx]
    pos_ref, neg_ref = refs[n_emb + n_ctx : n_emb + n_ctx + 2]
    outs = refs[n_emb + n_ctx + 2 : n_emb + n_ctx + 2 + n_gemb + n_gctx]
    gemb_refs, gctx_refs = outs[:n_gemb], outs[n_gemb:]
    acc_e, acc_ct, emb_t, emb_ref, ctx_ref = refs[n_emb + n_ctx + 2 + n_gemb + n_gctx :]
    k = pl.program_id(0)
    n = count_ref[0]

    @pl.when(k == 0)
    def _():
        at = 0
        for piece in emb_pieces:
            rows = piece.shape[0]
            emb_ref[at : at + rows, :] = piece[...]
            emb_t[:, at : at + rows] = piece[...].astype(jnp.float32).T.astype(emb_t.dtype)
            at += rows
        at = 0
        for piece in ctx_pieces:
            rows = piece.shape[0]
            ctx_ref[at : at + rows, :] = piece[...]
            at += rows
        acc_e[...] = jnp.zeros_like(acc_e)
        acc_ct[...] = jnp.zeros_like(acc_ct)

    def visit(j):
        slot = k * group + j
        r0 = pl.multiple_of(rows_ref[slot] * tile, tile)
        c0 = pl.multiple_of(cols_ref[slot] * tile, tile)
        e = emb_ref[pl.ds(r0, tile), :]
        c = ctx_ref[pl.ds(c0, tile), :]
        score = lax.dot_general(e, c, (((1,), (1,)), ((), ())), preferred_element_type=jnp.float32)
        positive = pos_ref[j].astype(jnp.float32)
        negative = neg_ref[j].astype(jnp.float32)
        t = jnp.tanh(score * 0.5)
        coeff = (0.5 * ((positive - negative) - (positive + negative) * t)).astype(jnp.bfloat16)
        acc_e[pl.ds(r0, tile), :] += jnp.dot(coeff, c, preferred_element_type=jnp.float32)
        acc_ct[:, pl.ds(c0, tile)] += jnp.dot(
            emb_t[:, pl.ds(r0, tile)], coeff, preferred_element_type=jnp.float32
        )

    full = (k + 1) * group <= n

    @pl.when(full)
    def _():
        for j in range(group):
            visit(j)

    @pl.when(jnp.logical_not(full))
    def _():
        for j in range(group):
            pl.when(k * group + j < n)(functools.partial(visit, j))

    @pl.when(k == pl.num_programs(0) - 1)
    def _():
        for p, out in enumerate(gemb_refs):
            rows = out.shape[0]
            out[...] = acc_e[p * rows : (p + 1) * rows, :].astype(out.dtype)
        for p, out in enumerate(gctx_refs):
            rows = out.shape[0]
            out[...] = acc_ct[:, p * rows : (p + 1) * rows].T.astype(out.dtype)


def tile_sweep(pos, neg, rows, cols, count, emb_pieces, ctx_pieces, n_gemb, n_gctx):
    cap, tile, _ = pos.shape
    dim = emb_pieces[0].shape[1]
    ne = sum(p.shape[0] for p in emb_pieces)
    nc = sum(p.shape[0] for p in ctx_pieces)
    group = next(g for g in (8, 4, 2, 1) if cap % g == 0)

    def slot(k, rows_ref, cols_ref, count_ref):
        last = jnp.maximum((count_ref[0] + group - 1) // group - 1, 0)
        return (jnp.minimum(k, last), 0, 0)

    grid_spec = pltpu.PrefetchScalarGridSpec(
        num_scalar_prefetch=3,
        grid=(cap // group,),
        in_specs=[pl.BlockSpec(p.shape, lambda k, *_: (0, 0)) for p in emb_pieces + ctx_pieces]
        + [
            pl.BlockSpec((group, tile, tile), slot),
            pl.BlockSpec((group, tile, tile), slot),
        ],
        out_specs=[pl.BlockSpec((ne // n_gemb, dim), lambda k, *_: (0, 0))] * n_gemb
        + [pl.BlockSpec((nc // n_gctx, dim), lambda k, *_: (0, 0))] * n_gctx,
        scratch_shapes=[
            pltpu.VMEM((ne, dim), jnp.float32),
            pltpu.VMEM((dim, nc), jnp.float32),
            pltpu.VMEM((dim, ne), jnp.bfloat16),
            pltpu.VMEM((ne, dim), jnp.bfloat16),
            pltpu.VMEM((nc, dim), jnp.bfloat16),
        ],
    )
    flops = cap * 3 * 2 * tile * tile * dim
    outs = pl.pallas_call(
        functools.partial(sweep_kernel, tile, group, len(emb_pieces), len(ctx_pieces), n_gemb, n_gctx),
        grid_spec=grid_spec,
        out_shape=[jax.ShapeDtypeStruct((ne // n_gemb, dim), jnp.bfloat16)] * n_gemb
        + [jax.ShapeDtypeStruct((nc // n_gctx, dim), jnp.bfloat16)] * n_gctx,
        compiler_params=pltpu.CompilerParams(dimension_semantics=("arbitrary",)),
        cost_estimate=pl.CostEstimate(
            flops=flops,
            transcendentals=cap * tile * tile,
            bytes_accessed=2 * cap * tile * tile * 2 + 3 * (ne + nc) * dim * 2,
        ),
    )(rows, cols, count.reshape(1), *emb_pieces, *ctx_pieces, pos, neg)
    return outs[:n_gemb], outs[n_gemb:]


def gather_rotated(x, axis, n):
    pieces = [x]
    for s in range(1, n):
        pieces.append(lax.ppermute(x, axis, [(i, (i + s) % n) for i in range(n)]))
    return pieces


def scatter_rotated(chunks, axis, n):
    total = chunks[0].astype(jnp.float32)
    for s in range(1, n):
        got = lax.ppermute(chunks[(n - s) % n], axis, [(i, (i + s) % n) for i in range(n)])
        total = total + got.astype(jnp.float32)
    return total


def paired(n):
    return n % 2 == 0 and n & (n - 1) == 0


def gather_paired(x, axis, n):
    pair = jnp.concatenate([x, lax.ppermute(x, axis, [(i, i ^ 1) for i in range(n)])], axis=0)
    blocks = [pair]
    for b in range(1, n // 2):
        blocks.append(lax.ppermute(pair, axis, [(i, i ^ (2 * b)) for i in range(n)]))
    return blocks


def scatter_paired(blocks, axis, n):
    total = blocks[0].astype(jnp.float32)
    for b in range(1, n // 2):
        got = lax.ppermute(blocks[b], axis, [(i, i ^ (2 * b)) for i in range(n)])
        total = total + got.astype(jnp.float32)
    width = total.shape[0] // 2
    got = lax.ppermute(total[width:], axis, [(i, i ^ 1) for i in range(n)])
    return total[:width] + got


def spread_pairs(pair, axis, n):
    blocks = [pair]
    for b in range(1, n // 2):
        blocks.append(lax.ppermute(pair, axis, [(i, i ^ (2 * b)) for i in range(n)]))
    return blocks


def reduce_pairs(blocks, axis, n):
    total = blocks[0].astype(jnp.float32)
    for b in range(1, n // 2):
        got = lax.ppermute(blocks[b], axis, [(i, i ^ (2 * b)) for i in range(n)])
        total = total + got.astype(jnp.float32)
    width = total.shape[0] // 2
    other = lax.ppermute(total, axis, [(i, i ^ 1) for i in range(n)])
    return total + jnp.concatenate([other[width:], other[:width]], axis=0)


def gather_xor(x, axis, n):
    pieces = [x]
    for p in range(1, n):
        pieces.append(lax.ppermute(x, axis, [(i, i ^ p) for i in range(n)]))
    return pieces


def scatter_xor(chunks, axis, n):
    total = chunks[0].astype(jnp.float32)
    for p in range(1, n):
        got = lax.ppermute(chunks[p], axis, [(i, i ^ p) for i in range(n)])
        total = total + got.astype(jnp.float32)
    return total


def pair_index(index, me, per_run):
    return (me ^ (index // per_run)) * per_run + index % per_run


def rotate_index(index, me, n, per_run):
    run = index // per_run
    return ((me - run) % n) * per_run + index % per_run


def body(emb_in, ctx_in, pos_weight, neg_weight, tile_row, tile_col, tile_count):
    n_row = lax.axis_size("row")
    n_col = lax.axis_size("col")
    me_row = lax.axis_index("row")
    me_col = lax.axis_index("col")
    pos = pos_weight[0, 0]
    neg = neg_weight[0, 0]
    tile = pos.shape[-1]
    per_run = emb_in.shape[0] // tile
    rows = rotate_index(tile_row[0, 0], me_col, n_col, per_run)
    if paired(n_row):
        cols = pair_index(tile_col[0, 0], me_row, per_run)
        gathers = (gather_paired, gather_xor)
        scatters = (scatter_paired, scatter_paired)
        splits = (n_row // 2, n_row // 2)
    else:
        cols = rotate_index(tile_col[0, 0], me_row, n_row, per_run)
        gathers = (gather_rotated, gather_rotated)
        scatters = (scatter_rotated, scatter_rotated)
        splits = (n_row, n_row)
    count = tile_count[0, 0]
    width = ctx_in.shape[0]
    emb = emb_in
    ctx = ctx_in
    pair = None
    for iteration in range(ITERS):
        first, last = iteration == 0, iteration == ITERS - 1
        emb_low = gather_rotated(emb.astype(jnp.bfloat16), "col", n_col)
        if not paired(n_row):
            ctx_low = gathers[0](ctx.astype(jnp.bfloat16), "row", n_row)
        else:
            if first:
                partner = lax.ppermute(ctx, "row", [(i, i ^ 1) for i in range(n_row)])
                pair = jnp.concatenate([ctx, partner], axis=0)
            ctx_low = spread_pairs(pair.astype(jnp.bfloat16), "row", n_row)
        grad_emb, grad_ctx = tile_sweep(
            pos, neg, rows, cols, count, emb_low, ctx_low, n_col, splits[1 if last else 0]
        )
        emb = emb + 0.05 * scatter_rotated(grad_emb, "col", n_col)
        if not paired(n_row):
            ctx = ctx + 0.05 * scatters[0](grad_ctx, "row", n_row)
        elif last:
            ctx = pair[:width] + 0.05 * scatter_paired(grad_ctx, "row", n_row)
        else:
            pair = pair + 0.05 * reduce_pairs(grad_ctx, "row", n_row)
    return (emb, ctx)


def solution(mesh):
    in_specs = (
        P(("row", "col"), None),
        P(("row", "col"), None),
        P("row", "col", None, None, None),
        P("row", "col", None, None, None),
        P("row", "col", None),
        P("row", "col", None),
        P("row", "col"),
    )
    out_specs = (P(("row", "col"), None), P(("row", "col"), None))
    return jax.shard_map(body, mesh=mesh, in_specs=in_specs, out_specs=out_specs, check_vma=False)
```

```python
import functools

import jax
import jax.numpy as jnp
from jax import lax
from jax.experimental import pallas as pl
from jax.experimental.pallas import tpu as pltpu
from jax.sharding import PartitionSpec as P

ITERS = 2


def sweep_kernel(tile, group, n_emb, n_ctx, n_gemb, n_gctx, rows_ref, cols_ref, count_ref, *refs):
    emb_pieces = refs[:n_emb]
    ctx_pieces = refs[n_emb : n_emb + n_ctx]
    pos_ref, neg_ref = refs[n_emb + n_ctx : n_emb + n_ctx + 2]
    outs = refs[n_emb + n_ctx + 2 : n_emb + n_ctx + 2 + n_gemb + n_gctx]
    gemb_refs, gctx_refs = outs[:n_gemb], outs[n_gemb:]
    acc_e, acc_ct, emb_t, emb_ref, ctx_ref = refs[n_emb + n_ctx + 2 + n_gemb + n_gctx :]
    k = pl.program_id(0)
    n = count_ref[0]

    @pl.when(k == 0)
    def _():
        at = 0
        for piece in emb_pieces:
            rows = piece.shape[0]
            emb_ref[at : at + rows, :] = piece[...]
            emb_t[:, at : at + rows] = piece[...].astype(jnp.float32).T.astype(emb_t.dtype)
            at += rows
        at = 0
        for piece in ctx_pieces:
            rows = piece.shape[0]
            ctx_ref[at : at + rows, :] = piece[...]
            at += rows
        acc_e[...] = jnp.zeros_like(acc_e)
        acc_ct[...] = jnp.zeros_like(acc_ct)

    def visit(j):
        slot = k * group + j
        r0 = pl.multiple_of(rows_ref[slot] * tile, tile)
        c0 = pl.multiple_of(cols_ref[slot] * tile, tile)
        e = emb_ref[pl.ds(r0, tile), :]
        c = ctx_ref[pl.ds(c0, tile), :]
        score = lax.dot_general(e, c, (((1,), (1,)), ((), ())), preferred_element_type=jnp.float32)
        positive = pos_ref[j].astype(jnp.float32)
        negative = neg_ref[j].astype(jnp.float32)
        t = jnp.tanh(score * 0.5)
        coeff = (0.5 * ((positive - negative) - (positive + negative) * t)).astype(jnp.bfloat16)
        acc_e[pl.ds(r0, tile), :] += jnp.dot(coeff, c, preferred_element_type=jnp.float32)
        acc_ct[:, pl.ds(c0, tile)] += jnp.dot(
            emb_t[:, pl.ds(r0, tile)], coeff, preferred_element_type=jnp.float32
        )

    full = (k + 1) * group <= n

    @pl.when(full)
    def _():
        for j in range(group):
            visit(j)

    @pl.when(jnp.logical_not(full))
    def _():
        for j in range(group):
            pl.when(k * group + j < n)(functools.partial(visit, j))

    @pl.when(k == pl.num_programs(0) - 1)
    def _():
        for p, out in enumerate(gemb_refs):
            rows = out.shape[0]
            out[...] = acc_e[p * rows : (p + 1) * rows, :].astype(out.dtype)
        for p, out in enumerate(gctx_refs):
            rows = out.shape[0]
            out[...] = acc_ct[:, p * rows : (p + 1) * rows].T.astype(out.dtype)


def tile_sweep(pos, neg, rows, cols, count, emb_pieces, ctx_pieces, n_gemb, n_gctx):
    cap, tile, _ = pos.shape
    dim = emb_pieces[0].shape[1]
    ne = sum(p.shape[0] for p in emb_pieces)
    nc = sum(p.shape[0] for p in ctx_pieces)
    group = next(g for g in (8, 4, 2, 1) if cap % g == 0)

    def slot(k, rows_ref, cols_ref, count_ref):
        last = jnp.maximum((count_ref[0] + group - 1) // group - 1, 0)
        return (jnp.minimum(k, last), 0, 0)

    grid_spec = pltpu.PrefetchScalarGridSpec(
        num_scalar_prefetch=3,
        grid=(cap // group,),
        in_specs=[pl.BlockSpec(p.shape, lambda k, *_: (0, 0)) for p in emb_pieces + ctx_pieces]
        + [
            pl.BlockSpec((group, tile, tile), slot),
            pl.BlockSpec((group, tile, tile), slot),
        ],
        out_specs=[pl.BlockSpec((ne // n_gemb, dim), lambda k, *_: (0, 0))] * n_gemb
        + [pl.BlockSpec((nc // n_gctx, dim), lambda k, *_: (0, 0))] * n_gctx,
        scratch_shapes=[
            pltpu.VMEM((ne, dim), jnp.float32),
            pltpu.VMEM((dim, nc), jnp.float32),
            pltpu.VMEM((dim, ne), jnp.bfloat16),
            pltpu.VMEM((ne, dim), jnp.bfloat16),
            pltpu.VMEM((nc, dim), jnp.bfloat16),
        ],
    )
    flops = cap * 3 * 2 * tile * tile * dim
    outs = pl.pallas_call(
        functools.partial(sweep_kernel, tile, group, len(emb_pieces), len(ctx_pieces), n_gemb, n_gctx),
        grid_spec=grid_spec,
        out_shape=[jax.ShapeDtypeStruct((ne // n_gemb, dim), jnp.bfloat16)] * n_gemb
        + [jax.ShapeDtypeStruct((nc // n_gctx, dim), jnp.bfloat16)] * n_gctx,
        compiler_params=pltpu.CompilerParams(dimension_semantics=("arbitrary",)),
        cost_estimate=pl.CostEstimate(
            flops=flops,
            transcendentals=cap * tile * tile,
            bytes_accessed=2 * cap * tile * tile * 2 + 3 * (ne + nc) * dim * 2,
        ),
    )(rows, cols, count.reshape(1), *emb_pieces, *ctx_pieces, pos, neg)
    return outs[:n_gemb], outs[n_gemb:]


def gather_rotated(x, axis, n):
    pieces = [x]
    for s in range(1, n):
        pieces.append(lax.ppermute(x, axis, [(i, (i + s) % n) for i in range(n)]))
    return pieces


def scatter_rotated(chunks, axis, n):
    total = chunks[0].astype(jnp.float32)
    for s in range(1, n):
        got = lax.ppermute(chunks[(n - s) % n], axis, [(i, (i + s) % n) for i in range(n)])
        total = total + got.astype(jnp.float32)
    return total


def paired(n):
    return n % 2 == 0 and n & (n - 1) == 0


def gather_paired(x, axis, n):
    pair = jnp.concatenate([x, lax.ppermute(x, axis, [(i, i ^ 1) for i in range(n)])], axis=0)
    blocks = [pair]
    for b in range(1, n // 2):
        blocks.append(lax.ppermute(pair, axis, [(i, i ^ (2 * b)) for i in range(n)]))
    return blocks


def scatter_paired(blocks, axis, n):
    total = blocks[0].astype(jnp.float32)
    for b in range(1, n // 2):
        got = lax.ppermute(blocks[b], axis, [(i, i ^ (2 * b)) for i in range(n)])
        total = total + got.astype(jnp.float32)
    width = total.shape[0] // 2
    got = lax.ppermute(total[width:], axis, [(i, i ^ 1) for i in range(n)])
    return total[:width] + got


def gather_xor(x, axis, n):
    pieces = [x]
    for p in range(1, n):
        pieces.append(lax.ppermute(x, axis, [(i, i ^ p) for i in range(n)]))
    return pieces


def scatter_xor(chunks, axis, n):
    total = chunks[0].astype(jnp.float32)
    for p in range(1, n):
        got = lax.ppermute(chunks[p], axis, [(i, i ^ p) for i in range(n)])
        total = total + got.astype(jnp.float32)
    return total


def pair_index(index, me, per_run):
    return (me ^ (index // per_run)) * per_run + index % per_run


def rotate_index(index, me, n, per_run):
    run = index // per_run
    return ((me - run) % n) * per_run + index % per_run


def body(emb_in, ctx_in, pos_weight, neg_weight, tile_row, tile_col, tile_count):
    n_row = lax.axis_size("row")
    n_col = lax.axis_size("col")
    me_row = lax.axis_index("row")
    me_col = lax.axis_index("col")
    pos = pos_weight[0, 0]
    neg = neg_weight[0, 0]
    tile = pos.shape[-1]
    per_run = emb_in.shape[0] // tile
    if paired(n_col):
        rows = pair_index(tile_row[0, 0], me_col, per_run)
        emb_gather, emb_scatters, emb_splits = gather_xor, (scatter_xor, scatter_paired), (n_col, n_col // 2)
    else:
        rows = rotate_index(tile_row[0, 0], me_col, n_col, per_run)
        emb_gather, emb_scatters, emb_splits = gather_rotated, (scatter_rotated, scatter_rotated), (n_col, n_col)
    if paired(n_row):
        cols = pair_index(tile_col[0, 0], me_row, per_run)
        gathers = (gather_paired, gather_xor)
        scatters = (scatter_paired, scatter_paired)
        splits = (n_row // 2, n_row // 2)
    else:
        cols = rotate_index(tile_col[0, 0], me_row, n_row, per_run)
        gathers = (gather_rotated, gather_rotated)
        scatters = (scatter_rotated, scatter_rotated)
        splits = (n_row, n_row)
    count = tile_count[0, 0]
    emb = emb_in
    ctx = ctx_in
    for iteration in range(ITERS):
        emb_low = emb_gather(emb.astype(jnp.bfloat16), "col", n_col)
        first, last = iteration == 0, iteration == ITERS - 1
        ctx_low = gathers[0 if first else 1](ctx.astype(jnp.bfloat16), "row", n_row)
        grad_emb, grad_ctx = tile_sweep(
            pos, neg, rows, cols, count, emb_low, ctx_low, emb_splits[1 if last else 0], splits[1 if last else 0]
        )
        emb = emb + 0.05 * emb_scatters[1 if last else 0](grad_emb, "col", n_col)
        ctx = ctx + 0.05 * scatters[1 if last else 0](grad_ctx, "row", n_row)
    return (emb, ctx)


def solution(mesh):
    in_specs = (
        P(("row", "col"), None),
        P(("row", "col"), None),
        P("row", "col", None, None, None),
        P("row", "col", None, None, None),
        P("row", "col", None),
        P("row", "col", None),
        P("row", "col"),
    )
    out_specs = (P(("row", "col"), None), P(("row", "col"), None))
    return jax.shard_map(body, mesh=mesh, in_specs=in_specs, out_specs=out_specs, check_vma=False)
```

```python
import functools

import jax
import jax.numpy as jnp
from jax import lax
from jax.experimental import pallas as pl
from jax.experimental.pallas import tpu as pltpu
from jax.sharding import PartitionSpec as P

ITERS = 2


def sweep_kernel(tile, group, n_emb, n_ctx, n_gemb, n_gctx, rows_ref, cols_ref, count_ref, *refs):
    emb_pieces = refs[:n_emb]
    ctx_pieces = refs[n_emb : n_emb + n_ctx]
    pos_ref, neg_ref = refs[n_emb + n_ctx : n_emb + n_ctx + 2]
    outs = refs[n_emb + n_ctx + 2 : n_emb + n_ctx + 2 + n_gemb + n_gctx]
    gemb_refs, gctx_refs = outs[:n_gemb], outs[n_gemb:]
    acc_e, acc_ct, emb_t, emb_ref, ctx_ref = refs[n_emb + n_ctx + 2 + n_gemb + n_gctx :]
    k = pl.program_id(0)
    n = count_ref[0]

    @pl.when(k == 0)
    def _():
        at = 0
        for piece in emb_pieces:
            rows = piece.shape[0]
            emb_ref[at : at + rows, :] = piece[...]
            emb_t[:, at : at + rows] = piece[...].astype(jnp.float32).T.astype(emb_t.dtype)
            at += rows
        at = 0
        for piece in ctx_pieces:
            rows = piece.shape[0]
            ctx_ref[at : at + rows, :] = piece[...]
            at += rows
        acc_e[...] = jnp.zeros_like(acc_e)
        acc_ct[...] = jnp.zeros_like(acc_ct)

    def visit(j):
        slot = k * group + j
        r0 = pl.multiple_of(rows_ref[slot] * tile, tile)
        c0 = pl.multiple_of(cols_ref[slot] * tile, tile)
        e = emb_ref[pl.ds(r0, tile), :]
        c = ctx_ref[pl.ds(c0, tile), :]
        score = lax.dot_general(e, c, (((1,), (1,)), ((), ())), preferred_element_type=jnp.float32)
        positive = pos_ref[j].astype(jnp.float32)
        negative = neg_ref[j].astype(jnp.float32)
        t = jnp.tanh(score * 0.5)
        coeff = (0.5 * ((positive - negative) - (positive + negative) * t)).astype(jnp.bfloat16)
        acc_e[pl.ds(r0, tile), :] += jnp.dot(coeff, c, preferred_element_type=jnp.float32)
        acc_ct[:, pl.ds(c0, tile)] += jnp.dot(
            emb_t[:, pl.ds(r0, tile)], coeff, preferred_element_type=jnp.float32
        )

    full = (k + 1) * group <= n

    @pl.when(full)
    def _():
        for j in range(group):
            visit(j)

    @pl.when(jnp.logical_not(full))
    def _():
        for j in range(group):
            pl.when(k * group + j < n)(functools.partial(visit, j))

    @pl.when(k == pl.num_programs(0) - 1)
    def _():
        for p, out in enumerate(gemb_refs):
            rows = out.shape[0]
            out[...] = acc_e[p * rows : (p + 1) * rows, :].astype(out.dtype)
        for p, out in enumerate(gctx_refs):
            rows = out.shape[0]
            out[...] = acc_ct[:, p * rows : (p + 1) * rows].T.astype(out.dtype)


def tile_sweep(pos, neg, rows, cols, count, emb_pieces, ctx_pieces, n_gemb, n_gctx):
    cap, tile, _ = pos.shape
    dim = emb_pieces[0].shape[1]
    ne = sum(p.shape[0] for p in emb_pieces)
    nc = sum(p.shape[0] for p in ctx_pieces)
    group = next(g for g in (8, 4, 2, 1) if cap % g == 0)

    def slot(k, rows_ref, cols_ref, count_ref):
        last = jnp.maximum((count_ref[0] + group - 1) // group - 1, 0)
        return (jnp.minimum(k, last), 0, 0)

    grid_spec = pltpu.PrefetchScalarGridSpec(
        num_scalar_prefetch=3,
        grid=(cap // group,),
        in_specs=[pl.BlockSpec(p.shape, lambda k, *_: (0, 0)) for p in emb_pieces + ctx_pieces]
        + [
            pl.BlockSpec((group, tile, tile), slot),
            pl.BlockSpec((group, tile, tile), slot),
        ],
        out_specs=[pl.BlockSpec((ne // n_gemb, dim), lambda k, *_: (0, 0))] * n_gemb
        + [pl.BlockSpec((nc // n_gctx, dim), lambda k, *_: (0, 0))] * n_gctx,
        scratch_shapes=[
            pltpu.VMEM((ne, dim), jnp.float32),
            pltpu.VMEM((dim, nc), jnp.float32),
            pltpu.VMEM((dim, ne), jnp.bfloat16),
            pltpu.VMEM((ne, dim), jnp.bfloat16),
            pltpu.VMEM((nc, dim), jnp.bfloat16),
        ],
    )
    flops = cap * 3 * 2 * tile * tile * dim
    outs = pl.pallas_call(
        functools.partial(sweep_kernel, tile, group, len(emb_pieces), len(ctx_pieces), n_gemb, n_gctx),
        grid_spec=grid_spec,
        out_shape=[jax.ShapeDtypeStruct((ne // n_gemb, dim), jnp.bfloat16)] * n_gemb
        + [jax.ShapeDtypeStruct((nc // n_gctx, dim), jnp.bfloat16)] * n_gctx,
        compiler_params=pltpu.CompilerParams(dimension_semantics=("arbitrary",)),
        cost_estimate=pl.CostEstimate(
            flops=flops,
            transcendentals=cap * tile * tile,
            bytes_accessed=2 * cap * tile * tile * 2 + 3 * (ne + nc) * dim * 2,
        ),
    )(rows, cols, count.reshape(1), *emb_pieces, *ctx_pieces, pos, neg)
    return outs[:n_gemb], outs[n_gemb:]


def gather_rotated(x, axis, n):
    pieces = [x]
    for s in range(1, n):
        pieces.append(lax.ppermute(x, axis, [(i, (i + s) % n) for i in range(n)]))
    return pieces


def scatter_rotated(chunks, axis, n):
    total = chunks[0].astype(jnp.float32)
    for s in range(1, n):
        got = lax.ppermute(chunks[(n - s) % n], axis, [(i, (i + s) % n) for i in range(n)])
        total = total + got.astype(jnp.float32)
    return total


def paired(n):
    return n % 2 == 0 and n & (n - 1) == 0


def gather_paired(x, axis, n):
    pair = jnp.concatenate([x, lax.ppermute(x, axis, [(i, i ^ 1) for i in range(n)])], axis=0)
    blocks = [pair]
    for b in range(1, n // 2):
        blocks.append(lax.ppermute(pair, axis, [(i, i ^ (2 * b)) for i in range(n)]))
    return blocks


def scatter_paired(blocks, axis, n):
    total = blocks[0].astype(jnp.float32)
    for b in range(1, n // 2):
        got = lax.ppermute(blocks[b], axis, [(i, i ^ (2 * b)) for i in range(n)])
        total = total + got.astype(jnp.float32)
    width = total.shape[0] // 2
    got = lax.ppermute(total[width:], axis, [(i, i ^ 1) for i in range(n)])
    return total[:width] + got


def gather_xor(x, axis, n):
    pieces = [x]
    for p in range(1, n):
        pieces.append(lax.ppermute(x, axis, [(i, i ^ p) for i in range(n)]))
    return pieces


def scatter_xor(chunks, axis, n):
    total = chunks[0].astype(jnp.float32)
    for p in range(1, n):
        got = lax.ppermute(chunks[p], axis, [(i, i ^ p) for i in range(n)])
        total = total + got.astype(jnp.float32)
    return total


def pair_index(index, me, per_run):
    return (me ^ (index // per_run)) * per_run + index % per_run


def rotate_index(index, me, n, per_run):
    run = index // per_run
    return ((me - run) % n) * per_run + index % per_run


def body(emb_in, ctx_in, pos_weight, neg_weight, tile_row, tile_col, tile_count):
    n_row = lax.axis_size("row")
    n_col = lax.axis_size("col")
    me_row = lax.axis_index("row")
    me_col = lax.axis_index("col")
    pos = pos_weight[0, 0]
    neg = neg_weight[0, 0]
    tile = pos.shape[-1]
    per_run = emb_in.shape[0] // tile
    rows = rotate_index(tile_row[0, 0], me_col, n_col, per_run)
    if paired(n_row):
        cols = pair_index(tile_col[0, 0], me_row, per_run)
        gathers = (gather_xor, gather_xor)
        scatters = (scatter_paired, scatter_paired)
        splits = (n_row // 2, n_row // 2)
    else:
        cols = rotate_index(tile_col[0, 0], me_row, n_row, per_run)
        gathers = (gather_rotated, gather_rotated)
        scatters = (scatter_rotated, scatter_rotated)
        splits = (n_row, n_row)
    count = tile_count[0, 0]
    emb = emb_in
    ctx = ctx_in
    for iteration in range(ITERS):
        emb_low = gather_rotated(emb.astype(jnp.bfloat16), "col", n_col)
        first, last = iteration == 0, iteration == ITERS - 1
        ctx_low = gathers[0 if first else 1](ctx.astype(jnp.bfloat16), "row", n_row)
        grad_emb, grad_ctx = tile_sweep(
            pos, neg, rows, cols, count, emb_low, ctx_low, n_col, splits[1 if last else 0]
        )
        emb = emb + 0.05 * scatter_rotated(grad_emb, "col", n_col)
        ctx = ctx + 0.05 * scatters[1 if last else 0](grad_ctx, "row", n_row)
    return (emb, ctx)


def solution(mesh):
    in_specs = (
        P(("row", "col"), None),
        P(("row", "col"), None),
        P("row", "col", None, None, None),
        P("row", "col", None, None, None),
        P("row", "col", None),
        P("row", "col", None),
        P("row", "col"),
    )
    out_specs = (P(("row", "col"), None), P(("row", "col"), None))
    return jax.shard_map(body, mesh=mesh, in_specs=in_specs, out_specs=out_specs, check_vma=False)
```

```python
import functools

import jax
import jax.numpy as jnp
from jax import lax
from jax.experimental import pallas as pl
from jax.experimental.pallas import tpu as pltpu
from jax.sharding import PartitionSpec as P

ITERS = 2


def sweep_kernel(tile, group, n_emb, n_ctx, n_gemb, n_gctx, rows_ref, cols_ref, count_ref, *refs):
    emb_pieces = refs[:n_emb]
    ctx_pieces = refs[n_emb : n_emb + n_ctx]
    pos_ref, neg_ref = refs[n_emb + n_ctx : n_emb + n_ctx + 2]
    outs = refs[n_emb + n_ctx + 2 : n_emb + n_ctx + 2 + n_gemb + n_gctx]
    gemb_refs, gctx_refs = outs[:n_gemb], outs[n_gemb:]
    acc_e, acc_ct, emb_t, emb_ref, ctx_ref = refs[n_emb + n_ctx + 2 + n_gemb + n_gctx :]
    k = pl.program_id(0)
    n = count_ref[0]

    @pl.when(k == 0)
    def _():
        at = 0
        for piece in emb_pieces:
            rows = piece.shape[0]
            emb_ref[at : at + rows, :] = (piece[...].astype(jnp.float32) * 0.5).astype(emb_ref.dtype)
            emb_t[:, at : at + rows] = piece[...].astype(jnp.float32).T.astype(emb_t.dtype)
            at += rows
        at = 0
        for piece in ctx_pieces:
            rows = piece.shape[0]
            ctx_ref[at : at + rows, :] = piece[...]
            at += rows
        acc_e[...] = jnp.zeros_like(acc_e)
        acc_ct[...] = jnp.zeros_like(acc_ct)

    def visit(j):
        slot = k * group + j
        r0 = pl.multiple_of(rows_ref[slot] * tile, tile)
        c0 = pl.multiple_of(cols_ref[slot] * tile, tile)
        e = emb_ref[pl.ds(r0, tile), :]
        c = ctx_ref[pl.ds(c0, tile), :]
        score = lax.dot_general(e, c, (((1,), (1,)), ((), ())), preferred_element_type=jnp.float32)
        positive = pos_ref[j].astype(jnp.float32)
        negative = neg_ref[j].astype(jnp.float32)
        t = jnp.tanh(score)
        coeff = (0.5 * ((positive - negative) - (positive + negative) * t)).astype(jnp.bfloat16)
        acc_e[pl.ds(r0, tile), :] += jnp.dot(coeff, c, preferred_element_type=jnp.float32)
        acc_ct[:, pl.ds(c0, tile)] += jnp.dot(
            emb_t[:, pl.ds(r0, tile)], coeff, preferred_element_type=jnp.float32
        )

    full = (k + 1) * group <= n

    @pl.when(full)
    def _():
        for j in range(group):
            visit(j)

    @pl.when(jnp.logical_not(full))
    def _():
        for j in range(group):
            pl.when(k * group + j < n)(functools.partial(visit, j))

    @pl.when(k == pl.num_programs(0) - 1)
    def _():
        for p, out in enumerate(gemb_refs):
            rows = out.shape[0]
            out[...] = acc_e[p * rows : (p + 1) * rows, :].astype(out.dtype)
        for p, out in enumerate(gctx_refs):
            rows = out.shape[0]
            out[...] = acc_ct[:, p * rows : (p + 1) * rows].T.astype(out.dtype)


def tile_sweep(pos, neg, rows, cols, count, emb_pieces, ctx_pieces, n_gemb, n_gctx):
    cap, tile, _ = pos.shape
    dim = emb_pieces[0].shape[1]
    ne = sum(p.shape[0] for p in emb_pieces)
    nc = sum(p.shape[0] for p in ctx_pieces)
    group = next(g for g in (8, 4, 2, 1) if cap % g == 0)

    def slot(k, rows_ref, cols_ref, count_ref):
        last = jnp.maximum((count_ref[0] + group - 1) // group - 1, 0)
        return (jnp.minimum(k, last), 0, 0)

    grid_spec = pltpu.PrefetchScalarGridSpec(
        num_scalar_prefetch=3,
        grid=(cap // group,),
        in_specs=[pl.BlockSpec(p.shape, lambda k, *_: (0, 0)) for p in emb_pieces + ctx_pieces]
        + [
            pl.BlockSpec((group, tile, tile), slot),
            pl.BlockSpec((group, tile, tile), slot),
        ],
        out_specs=[pl.BlockSpec((ne // n_gemb, dim), lambda k, *_: (0, 0))] * n_gemb
        + [pl.BlockSpec((nc // n_gctx, dim), lambda k, *_: (0, 0))] * n_gctx,
        scratch_shapes=[
            pltpu.VMEM((ne, dim), jnp.float32),
            pltpu.VMEM((dim, nc), jnp.float32),
            pltpu.VMEM((dim, ne), jnp.bfloat16),
            pltpu.VMEM((ne, dim), jnp.bfloat16),
            pltpu.VMEM((nc, dim), jnp.bfloat16),
        ],
    )
    flops = cap * 3 * 2 * tile * tile * dim
    outs = pl.pallas_call(
        functools.partial(sweep_kernel, tile, group, len(emb_pieces), len(ctx_pieces), n_gemb, n_gctx),
        grid_spec=grid_spec,
        out_shape=[jax.ShapeDtypeStruct((ne // n_gemb, dim), jnp.bfloat16)] * n_gemb
        + [jax.ShapeDtypeStruct((nc // n_gctx, dim), jnp.bfloat16)] * n_gctx,
        compiler_params=pltpu.CompilerParams(dimension_semantics=("arbitrary",)),
        cost_estimate=pl.CostEstimate(
            flops=flops,
            transcendentals=cap * tile * tile,
            bytes_accessed=2 * cap * tile * tile * 2 + 3 * (ne + nc) * dim * 2,
        ),
    )(rows, cols, count.reshape(1), *emb_pieces, *ctx_pieces, pos, neg)
    return outs[:n_gemb], outs[n_gemb:]


def gather_rotated(x, axis, n):
    pieces = [x]
    for s in range(1, n):
        pieces.append(lax.ppermute(x, axis, [(i, (i + s) % n) for i in range(n)]))
    return pieces


def scatter_rotated(chunks, axis, n):
    total = chunks[0].astype(jnp.float32)
    for s in range(1, n):
        got = lax.ppermute(chunks[(n - s) % n], axis, [(i, (i + s) % n) for i in range(n)])
        total = total + got.astype(jnp.float32)
    return total


def paired(n):
    return n % 2 == 0 and n & (n - 1) == 0


def gather_paired(x, axis, n):
    pair = jnp.concatenate([x, lax.ppermute(x, axis, [(i, i ^ 1) for i in range(n)])], axis=0)
    blocks = [pair]
    for b in range(1, n // 2):
        blocks.append(lax.ppermute(pair, axis, [(i, i ^ (2 * b)) for i in range(n)]))
    return blocks


def scatter_paired(blocks, axis, n):
    total = blocks[0].astype(jnp.float32)
    for b in range(1, n // 2):
        got = lax.ppermute(blocks[b], axis, [(i, i ^ (2 * b)) for i in range(n)])
        total = total + got.astype(jnp.float32)
    width = total.shape[0] // 2
    got = lax.ppermute(total[width:], axis, [(i, i ^ 1) for i in range(n)])
    return total[:width] + got


def gather_xor(x, axis, n):
    pieces = [x]
    for p in range(1, n):
        pieces.append(lax.ppermute(x, axis, [(i, i ^ p) for i in range(n)]))
    return pieces


def scatter_xor(chunks, axis, n):
    total = chunks[0].astype(jnp.float32)
    for p in range(1, n):
        got = lax.ppermute(chunks[p], axis, [(i, i ^ p) for i in range(n)])
        total = total + got.astype(jnp.float32)
    return total


def pair_index(index, me, per_run):
    return (me ^ (index // per_run)) * per_run + index % per_run


def rotate_index(index, me, n, per_run):
    run = index // per_run
    return ((me - run) % n) * per_run + index % per_run


def body(emb_in, ctx_in, pos_weight, neg_weight, tile_row, tile_col, tile_count):
    n_row = lax.axis_size("row")
    n_col = lax.axis_size("col")
    me_row = lax.axis_index("row")
    me_col = lax.axis_index("col")
    pos = pos_weight[0, 0]
    neg = neg_weight[0, 0]
    tile = pos.shape[-1]
    per_run = emb_in.shape[0] // tile
    rows = rotate_index(tile_row[0, 0], me_col, n_col, per_run)
    if paired(n_row):
        cols = pair_index(tile_col[0, 0], me_row, per_run)
        gathers = (gather_paired, gather_xor)
        scatters = (scatter_paired, scatter_paired)
        splits = (n_row // 2, n_row // 2)
    else:
        cols = rotate_index(tile_col[0, 0], me_row, n_row, per_run)
        gathers = (gather_rotated, gather_rotated)
        scatters = (scatter_rotated, scatter_rotated)
        splits = (n_row, n_row)
    count = tile_count[0, 0]
    emb = emb_in
    ctx = ctx_in
    for iteration in range(ITERS):
        emb_low = gather_rotated(emb.astype(jnp.bfloat16), "col", n_col)
        first, last = iteration == 0, iteration == ITERS - 1
        ctx_low = gathers[0 if first else 1](ctx.astype(jnp.bfloat16), "row", n_row)
        grad_emb, grad_ctx = tile_sweep(
            pos, neg, rows, cols, count, emb_low, ctx_low, n_col, splits[1 if last else 0]
        )
        emb = emb + 0.05 * scatter_rotated(grad_emb, "col", n_col)
        ctx = ctx + 0.05 * scatters[1 if last else 0](grad_ctx, "row", n_row)
    return (emb, ctx)


def solution(mesh):
    in_specs = (
        P(("row", "col"), None),
        P(("row", "col"), None),
        P("row", "col", None, None, None),
        P("row", "col", None, None, None),
        P("row", "col", None),
        P("row", "col", None),
        P("row", "col"),
    )
    out_specs = (P(("row", "col"), None), P(("row", "col"), None))
    return jax.shard_map(body, mesh=mesh, in_specs=in_specs, out_specs=out_specs, check_vma=False)
```

```python
import functools

import jax
import jax.numpy as jnp
from jax import lax
from jax.experimental import pallas as pl
from jax.experimental.pallas import tpu as pltpu
from jax.sharding import PartitionSpec as P

ITERS = 2


def sweep_kernel(tile, group, n_emb, n_ctx, n_gemb, n_gctx, rows_ref, cols_ref, count_ref, *refs):
    emb_pieces = refs[:n_emb]
    ctx_pieces = refs[n_emb : n_emb + n_ctx]
    pos_ref, neg_ref = refs[n_emb + n_ctx : n_emb + n_ctx + 2]
    outs = refs[n_emb + n_ctx + 2 : n_emb + n_ctx + 2 + n_gemb + n_gctx]
    gemb_refs, gctx_refs = outs[:n_gemb], outs[n_gemb:]
    acc_e, acc_ct, emb_t, emb_ref, ctx_ref = refs[n_emb + n_ctx + 2 + n_gemb + n_gctx :]
    k = pl.program_id(0)
    n = count_ref[0]

    @pl.when(k == 0)
    def _():
        at = 0
        for piece in emb_pieces:
            rows = piece.shape[0]
            emb_ref[at : at + rows, :] = piece[...]
            emb_t[:, at : at + rows] = (piece[...].astype(jnp.float32) * 0.5).T.astype(emb_t.dtype)
            at += rows
        at = 0
        for piece in ctx_pieces:
            rows = piece.shape[0]
            ctx_ref[at : at + rows, :] = (piece[...].astype(jnp.float32) * 0.5).astype(ctx_ref.dtype)
            at += rows
        acc_e[...] = jnp.zeros_like(acc_e)
        acc_ct[...] = jnp.zeros_like(acc_ct)

    def visit(j):
        slot = k * group + j
        r0 = pl.multiple_of(rows_ref[slot] * tile, tile)
        c0 = pl.multiple_of(cols_ref[slot] * tile, tile)
        e = emb_ref[pl.ds(r0, tile), :]
        c = ctx_ref[pl.ds(c0, tile), :]
        score = lax.dot_general(e, c, (((1,), (1,)), ((), ())), preferred_element_type=jnp.float32)
        positive = pos_ref[j].astype(jnp.float32)
        negative = neg_ref[j].astype(jnp.float32)
        t = jnp.tanh(score)
        coeff = ((positive - negative) - (positive + negative) * t).astype(jnp.bfloat16)
        acc_e[pl.ds(r0, tile), :] += jnp.dot(coeff, c, preferred_element_type=jnp.float32)
        acc_ct[:, pl.ds(c0, tile)] += jnp.dot(
            emb_t[:, pl.ds(r0, tile)], coeff, preferred_element_type=jnp.float32
        )

    full = (k + 1) * group <= n

    @pl.when(full)
    def _():
        for j in range(group):
            visit(j)

    @pl.when(jnp.logical_not(full))
    def _():
        for j in range(group):
            pl.when(k * group + j < n)(functools.partial(visit, j))

    @pl.when(k == pl.num_programs(0) - 1)
    def _():
        for p, out in enumerate(gemb_refs):
            rows = out.shape[0]
            out[...] = acc_e[p * rows : (p + 1) * rows, :].astype(out.dtype)
        for p, out in enumerate(gctx_refs):
            rows = out.shape[0]
            out[...] = acc_ct[:, p * rows : (p + 1) * rows].T.astype(out.dtype)


def tile_sweep(pos, neg, rows, cols, count, emb_pieces, ctx_pieces, n_gemb, n_gctx):
    cap, tile, _ = pos.shape
    dim = emb_pieces[0].shape[1]
    ne = sum(p.shape[0] for p in emb_pieces)
    nc = sum(p.shape[0] for p in ctx_pieces)
    group = next(g for g in (8, 4, 2, 1) if cap % g == 0)

    def slot(k, rows_ref, cols_ref, count_ref):
        last = jnp.maximum((count_ref[0] + group - 1) // group - 1, 0)
        return (jnp.minimum(k, last), 0, 0)

    grid_spec = pltpu.PrefetchScalarGridSpec(
        num_scalar_prefetch=3,
        grid=(cap // group,),
        in_specs=[pl.BlockSpec(p.shape, lambda k, *_: (0, 0)) for p in emb_pieces + ctx_pieces]
        + [
            pl.BlockSpec((group, tile, tile), slot),
            pl.BlockSpec((group, tile, tile), slot),
        ],
        out_specs=[pl.BlockSpec((ne // n_gemb, dim), lambda k, *_: (0, 0))] * n_gemb
        + [pl.BlockSpec((nc // n_gctx, dim), lambda k, *_: (0, 0))] * n_gctx,
        scratch_shapes=[
            pltpu.VMEM((ne, dim), jnp.float32),
            pltpu.VMEM((dim, nc), jnp.float32),
            pltpu.VMEM((dim, ne), jnp.bfloat16),
            pltpu.VMEM((ne, dim), jnp.bfloat16),
            pltpu.VMEM((nc, dim), jnp.bfloat16),
        ],
    )
    flops = cap * 3 * 2 * tile * tile * dim
    outs = pl.pallas_call(
        functools.partial(sweep_kernel, tile, group, len(emb_pieces), len(ctx_pieces), n_gemb, n_gctx),
        grid_spec=grid_spec,
        out_shape=[jax.ShapeDtypeStruct((ne // n_gemb, dim), jnp.bfloat16)] * n_gemb
        + [jax.ShapeDtypeStruct((nc // n_gctx, dim), jnp.bfloat16)] * n_gctx,
        compiler_params=pltpu.CompilerParams(dimension_semantics=("arbitrary",)),
        cost_estimate=pl.CostEstimate(
            flops=flops,
            transcendentals=cap * tile * tile,
            bytes_accessed=2 * cap * tile * tile * 2 + 3 * (ne + nc) * dim * 2,
        ),
    )(rows, cols, count.reshape(1), *emb_pieces, *ctx_pieces, pos, neg)
    return outs[:n_gemb], outs[n_gemb:]


def gather_rotated(x, axis, n):
    pieces = [x]
    for s in range(1, n):
        pieces.append(lax.ppermute(x, axis, [(i, (i + s) % n) for i in range(n)]))
    return pieces


def scatter_rotated(chunks, axis, n):
    total = chunks[0].astype(jnp.float32)
    for s in range(1, n):
        got = lax.ppermute(chunks[(n - s) % n], axis, [(i, (i + s) % n) for i in range(n)])
        total = total + got.astype(jnp.float32)
    return total


def paired(n):
    return n % 2 == 0 and n & (n - 1) == 0


def gather_paired(x, axis, n):
    pair = jnp.concatenate([x, lax.ppermute(x, axis, [(i, i ^ 1) for i in range(n)])], axis=0)
    blocks = [pair]
    for b in range(1, n // 2):
        blocks.append(lax.ppermute(pair, axis, [(i, i ^ (2 * b)) for i in range(n)]))
    return blocks


def scatter_paired(blocks, axis, n):
    total = blocks[0].astype(jnp.float32)
    for b in range(1, n // 2):
        got = lax.ppermute(blocks[b], axis, [(i, i ^ (2 * b)) for i in range(n)])
        total = total + got.astype(jnp.float32)
    width = total.shape[0] // 2
    got = lax.ppermute(total[width:], axis, [(i, i ^ 1) for i in range(n)])
    return total[:width] + got


def gather_xor(x, axis, n):
    pieces = [x]
    for p in range(1, n):
        pieces.append(lax.ppermute(x, axis, [(i, i ^ p) for i in range(n)]))
    return pieces


def scatter_xor(chunks, axis, n):
    total = chunks[0].astype(jnp.float32)
    for p in range(1, n):
        got = lax.ppermute(chunks[p], axis, [(i, i ^ p) for i in range(n)])
        total = total + got.astype(jnp.float32)
    return total


def pair_index(index, me, per_run):
    return (me ^ (index // per_run)) * per_run + index % per_run


def rotate_index(index, me, n, per_run):
    run = index // per_run
    return ((me - run) % n) * per_run + index % per_run


def body(emb_in, ctx_in, pos_weight, neg_weight, tile_row, tile_col, tile_count):
    n_row = lax.axis_size("row")
    n_col = lax.axis_size("col")
    me_row = lax.axis_index("row")
    me_col = lax.axis_index("col")
    pos = pos_weight[0, 0]
    neg = neg_weight[0, 0]
    tile = pos.shape[-1]
    per_run = emb_in.shape[0] // tile
    rows = rotate_index(tile_row[0, 0], me_col, n_col, per_run)
    if paired(n_row):
        cols = pair_index(tile_col[0, 0], me_row, per_run)
        gathers = (gather_paired, gather_xor)
        scatters = (scatter_paired, scatter_paired)
        splits = (n_row // 2, n_row // 2)
    else:
        cols = rotate_index(tile_col[0, 0], me_row, n_row, per_run)
        gathers = (gather_rotated, gather_rotated)
        scatters = (scatter_rotated, scatter_rotated)
        splits = (n_row, n_row)
    count = tile_count[0, 0]
    emb = emb_in
    ctx = ctx_in
    for iteration in range(ITERS):
        emb_low = gather_rotated(emb.astype(jnp.bfloat16), "col", n_col)
        first, last = iteration == 0, iteration == ITERS - 1
        ctx_low = gathers[0 if first else 1](ctx.astype(jnp.bfloat16), "row", n_row)
        grad_emb, grad_ctx = tile_sweep(
            pos, neg, rows, cols, count, emb_low, ctx_low, n_col, splits[1 if last else 0]
        )
        emb = emb + 0.05 * scatter_rotated(grad_emb, "col", n_col)
        ctx = ctx + 0.05 * scatters[1 if last else 0](grad_ctx, "row", n_row)
    return (emb, ctx)


def solution(mesh):
    in_specs = (
        P(("row", "col"), None),
        P(("row", "col"), None),
        P("row", "col", None, None, None),
        P("row", "col", None, None, None),
        P("row", "col", None),
        P("row", "col", None),
        P("row", "col"),
    )
    out_specs = (P(("row", "col"), None), P(("row", "col"), None))
    return jax.shard_map(body, mesh=mesh, in_specs=in_specs, out_specs=out_specs, check_vma=False)
```
